128 devices in a mesh: wave: 8 (over z_lo, x), strip: 16 (over y, z_hi, core).
Axes of the slice: x: 4, y: 4, z: 4 (z_hi: 2, z_lo: 2; z = z_hi * 2 + z_lo), core: 2. Of those that a mesh axis runs over, the one named last changes fastest.
Arguments:
- unit_params: float32 [9, 16, 24576], P(None, 'strip', 'wave'), may hold values from 0 to 1
- observed: bfloat16 [4, 256, 1536, 256], P(None, 'wave', 'strip'), may hold values from -3 to 3
- psf_rows: bfloat16 [256, 4, 65], P('wave'), may hold values from -0.75 to 0.75
- psf_cols: bfloat16 [256, 4, 65], P('wave'), may hold values from -0.75 to 0.75
- pixel_mask: int32 [1536, 256], P('strip'), may hold values 0 or 1
- strip_lengths: int32 [16], P('strip'), may hold values from 32 to 96, as said below
Outputs:
- param_grad: float32 [9, 16, 24576], P(None, 'strip', 'wave')
The draws below stay inside these ranges and needn't reach their ends.
Inputs may be any that keep to these rules, and one draw needn't show every extreme that they name: `strip_lengths`: the strip lengths sum to 1024; in every draw one strip holds 96 rows and one holds 32.
All inputs are finite; a program needn't handle non-finite values. No bound on the sum of `pixel_mask` on one device may be relied on, other than what follows from the above.
Results may differ from the reference program's by a relative error of at most 0.00098.
Values may be sent and summed in bfloat16 or wider, within the bound.
No kernel may reach another device: no remote copies, remote signals or barrier semaphores. Data moves between devices by JAX's collectives and lax.ppermute only.
A program may use at most 192 MiB of HBM per device.

```python
import jax
import jax.numpy as jnp
from jax import lax

STOKES = 4
NW = 256
PARAMS = 9
RANK = 4
HALF = 32
MEAN_ROWS = 64
COLS = 256
TAPS = 65
CAP = 96
STRIPS = 16
ROWS = 1024


def draw_unit_params(key, part):
    shape = (PARAMS, STRIPS, CAP * COLS)
    broad_key = jax.random.fold_in(key, 21)
    narrow_key = jax.random.fold_in(key, 22)
    broad = jax.random.uniform(broad_key, shape, jnp.float32, 0.0, 1.0)
    narrow = jax.random.uniform(narrow_key, shape, jnp.float32, 0.0, 1.0)
    narrow = 0.05 * narrow
    row_number = lax.broadcasted_iota(jnp.int32, shape, 0)
    is_narrow = (row_number == 4) | (row_number == 5)
    return jnp.where(is_narrow, narrow, broad).astype(jnp.float32)


def draw_strip_lengths(key, part):
    pair_count = STRIPS // 2
    first_key = jax.random.fold_in(key, 11)
    second_key = jax.random.fold_in(key, 12)
    third_key = jax.random.fold_in(key, 13)
    moved_rows = jax.random.randint(first_key, (pair_count,), -HALF, HALF + 1)
    chosen = jax.random.randint(second_key, (), 0, pair_count)
    moved_rows = jnp.where(jnp.arange(pair_count) == chosen, HALF, moved_rows).astype(jnp.int32)
    shuffled = jax.random.permutation(third_key, STRIPS)
    changes = jnp.zeros((STRIPS,), jnp.int32).at[shuffled[0::2]].add(moved_rows).at[shuffled[1::2]].add(-moved_rows)
    return (MEAN_ROWS + changes).astype(jnp.int32)


def with_ends(entries, key, low, high):
    longest = entries.shape.index(max(entries.shape))
    spots = []
    for shift in (0, 1):
        where = [jax.random.randint(jax.random.fold_in(key, axis), (), 0, length) for axis, length in enumerate(entries.shape)]
        where[longest] = (where[longest] + shift) % entries.shape[longest]
        spots.append(tuple(where))
    return entries.at[spots[0]].set(low).at[spots[1]].set(high)


def shard_levels(rng, dims, pieces, smallest, top_value):
    loudness, own = 1.0, jax.random.fold_in(rng, 6)
    for dim, blocks in pieces:
        steps = jnp.exp(jax.random.uniform(jax.random.fold_in(own, dim), (blocks,), jnp.float32, smallest / len(pieces), top_value / len(pieces)))
        loudness = loudness * jnp.repeat(steps, dims[dim] // blocks).reshape([-1 if axis == dim else 1 for axis in range(len(dims))])
    return loudness


def centred(rng, shape, width, limit, cuts=(), kind=jnp.bfloat16):
    entries = width * jax.random.normal(rng, shape, jnp.float32)
    if cuts:
        entries = entries * shard_levels(rng, shape, cuts, -0.22, 0.18)
    return jnp.clip(entries, -limit, limit).astype(kind)


def setup_inputs(seed: int = 0) -> dict:
    arg_keys = jax.random.split(jax.random.key(seed), 7)
    return {
        "unit_params": draw_unit_params(jax.random.fold_in(arg_keys[6], 71), 0),
        "observed": centred(arg_keys[1], (STOKES, NW, STRIPS * CAP, COLS), 0.5, 3.0, ((1, 8), (2, 16))),
        "psf_rows": centred(arg_keys[2], (NW, RANK, TAPS), TAPS ** -0.5, 0.75, ((0, 8),)),
        "psf_cols": centred(arg_keys[3], (NW, RANK, TAPS), TAPS ** -0.5, 0.75, ((0, 8),)),
        "pixel_mask": with_ends((jax.random.randint(arg_keys[4], (STRIPS * CAP, COLS), 0, 8) < 7).astype(jnp.int32), jax.random.fold_in(arg_keys[4], 1), 0, 1),
        "strip_lengths": draw_strip_lengths(jax.random.fold_in(arg_keys[6], 71), 0),
    }


parameter_low = (0.2, 0.4, 2.0, -0.8, 0.4, 0.3, 0.0, 0.0, 0.0)
parameter_span = (0.4, 0.6, 18.0, 1.6, 0.8, 1.2, 1.5, 3.141592653589793, 3.141592653589793)
stokes_weight = (1.0, 3.0, 3.0, 2.0)
loss_scale = 0.03125

def profile(distance, damping):
    scaled = distance / damping
    return 1.0 / (1.0 + scaled * scaled)

def stokes_model(unit_params, wave_grid):
    physical = [parameter_low[number] + parameter_span[number] * unit_params[number] for number in range(9)]
    source_zero, source_slope, strength, doppler, line_width, damping, zeeman_split, incline, azimuth = physical
    offset = (wave_grid[:, None, None] - doppler) / line_width
    split_ratio = zeeman_split / line_width
    centre = profile(offset, damping)
    upper_line = profile(offset - split_ratio, damping)
    lower_line = profile(offset + split_ratio, damping)
    cosine = jnp.cos(incline)
    sine_value = jnp.sin(incline)
    sine_square = sine_value * sine_value
    absorb_total = 1.0 + strength * (centre * sine_square * 0.5 + (upper_line + lower_line) * (1.0 + cosine * cosine) * 0.25)
    linear = strength * (centre - 0.5 * (upper_line + lower_line)) * sine_square * 0.5
    linear_cosine = linear * jnp.cos(2.0 * azimuth)
    linear_sine = linear * jnp.sin(2.0 * azimuth)
    circular = strength * (lower_line - upper_line) * cosine * 0.5
    denominator = absorb_total * absorb_total - linear_cosine * linear_cosine - linear_sine * linear_sine - circular * circular
    source_ratio = source_slope / denominator
    return jnp.stack([source_zero + source_ratio * absorb_total, -source_ratio * linear_cosine, -source_ratio * linear_sine, -source_ratio * circular])

def correlate(field, tap_table, axis_index):
    extent = field.shape[axis_index]
    tap_count = tap_table.shape[1]
    radius = tap_count // 2
    period = 1 << (extent + tap_count).bit_length()
    kernel = jnp.zeros((tap_table.shape[0], period), jnp.float32)
    kernel = kernel.at[:, :radius + 1].set(tap_table[:, radius:]).at[:, period - radius:].set(tap_table[:, :radius])
    kernel_spec = jnp.conj(jnp.fft.rfft(kernel, axis=1))
    layout = [tap_table.shape[0]] + [1] * (field.ndim - 1)
    layout[axis_index] = period // 2 + 1
    field_spec = jnp.fft.rfft(field, n=period, axis=axis_index)
    result = jnp.fft.irfft(field_spec * kernel_spec.reshape(layout), n=period, axis=axis_index)
    return lax.slice_in_dim(result, 0, extent, axis=axis_index)

def map_rows(strip_lengths):
    strip_ends = jnp.cumsum(strip_lengths).astype(jnp.int32)
    strip_starts = (strip_ends - strip_lengths).astype(jnp.int32)
    map_index = jnp.arange(ROWS, dtype=jnp.int32)
    owner_strip = lax.optimization_barrier(jnp.sum((map_index[:, None] >= strip_ends[None, :]).astype(jnp.int32), axis=1)).astype(jnp.int32)
    return (owner_strip * CAP + map_index - strip_starts[owner_strip]).astype(jnp.int32)

def reference(unit_params, observed, psf_rows, psf_cols, pixel_mask, strip_lengths):
    padded_rows = map_rows(strip_lengths)
    unit_map = unit_params.reshape(PARAMS, STRIPS * CAP, COLS)[:, padded_rows]
    live_map = pixel_mask[padded_rows].astype(jnp.float32)
    weight_square = jnp.array(stokes_weight, jnp.float32)
    weight_square = weight_square * weight_square

    def one_wave(number, gradient_sum):
        position = number.astype(jnp.float32)
        wave_grid = (-3.0 + 6.0 * position / (NW - 1)).reshape(1)

        def model_of(params_now):
            return stokes_model(params_now, wave_grid)[:, 0]
        model_exact, pullback = jax.vjp(model_of, unit_map)
        model_rounded = model_exact.astype(jnp.bfloat16)
        rows_taps = lax.dynamic_index_in_dim(psf_rows, number, 0, keepdims=False).astype(jnp.float32)
        cols_taps = lax.dynamic_index_in_dim(psf_cols, number, 0, keepdims=False).astype(jnp.float32)
        row_pass = correlate(model_rounded.astype(jnp.float32)[None], rows_taps, 2).astype(jnp.bfloat16)
        blurred = lax.optimization_barrier(jnp.sum(correlate(row_pass.astype(jnp.float32), cols_taps, 3), axis=0))
        observed_map = lax.dynamic_index_in_dim(observed, number, 1, keepdims=False)[:, padded_rows].astype(jnp.float32)
        residual = (loss_scale * weight_square[:, None, None] * live_map * (blurred - observed_map)).astype(jnp.bfloat16)
        across = correlate(residual.astype(jnp.float32)[None], cols_taps[:, ::-1], 3).astype(jnp.bfloat16)
        adjoint = lax.optimization_barrier(jnp.sum(correlate(across.astype(jnp.float32), rows_taps[:, ::-1], 2), axis=0))
        return gradient_sum + pullback(adjoint)[0]
    gradient_map = lax.fori_loop(0, NW, one_wave, jnp.zeros(unit_map.shape, jnp.float32))
    gradient_padded = jnp.zeros((PARAMS, STRIPS * CAP, COLS), jnp.float32).at[:, padded_rows].set(gradient_map)
    return gradient_padded.reshape(PARAMS, STRIPS, CAP * COLS)
```

```python
import jax
import jax.numpy as jnp
from jax import lax
from jax.sharding import PartitionSpec as P

parameter_low = (0.2, 0.4, 2.0, -0.8, 0.4, 0.3, 0.0, 0.0, 0.0)
parameter_span = (0.4, 0.6, 18.0, 1.6, 0.8, 1.2, 1.5, 3.141592653589793, 3.141592653589793)
stokes_weight = (1.0, 3.0, 3.0, 2.0)
loss_scale = 0.03125


def passed_along(shard, axis, by):
    count = lax.axis_size(axis)
    pairs = [(i, i + by) for i in range(count) if 0 <= i + by < count]
    return lax.ppermute(shard, axis, pairs)


def exchange(shard, axis, bit):
    count = lax.axis_size(axis)
    pairs = [(i, i ^ bit) for i in range(count)]
    return lax.ppermute(shard, axis, pairs)


def gather_by_doubling(shard, axis):
    count = lax.axis_size(axis)
    position = lax.axis_index(axis)
    bit = 1
    while bit < count:
        other = exchange(shard, axis, bit)
        low_side = (position & bit) == 0
        shard = jnp.where(
            low_side,
            jnp.concatenate([shard, other], axis=0),
            jnp.concatenate([other, shard], axis=0),
        )
        bit *= 2
    return shard


def scatter_by_halving(pieces, axis):
    count = lax.axis_size(axis)
    position = lax.axis_index(axis)
    bit = count // 2
    while bit >= 1:
        half = pieces.shape[0] // 2
        high_side = ((position & bit) != 0).astype(jnp.int32)
        keep = lax.dynamic_slice_in_dim(pieces, high_side * half, half, 0)
        give = lax.dynamic_slice_in_dim(pieces, (1 - high_side) * half, half, 0)
        pieces = keep + exchange(give, axis, bit)
        bit //= 2
    return pieces[0]


def profile(distance, damping):
    scaled = distance / damping
    return 1.0 / (1.0 + scaled * scaled)


def stokes_model(unit_params, wave_grid):
    physical = [
        parameter_low[number] + parameter_span[number] * unit_params[number] for number in range(9)
    ]
    (
        source_zero,
        source_slope,
        strength,
        doppler,
        line_width,
        damping,
        zeeman_split,
        incline,
        azimuth,
    ) = physical
    offset = (wave_grid[:, None, None] - doppler) / line_width
    split_ratio = zeeman_split / line_width
    centre = profile(offset, damping)
    upper_line = profile(offset - split_ratio, damping)
    lower_line = profile(offset + split_ratio, damping)
    cosine = jnp.cos(incline)
    sine_value = jnp.sin(incline)
    sine_square = sine_value * sine_value
    absorb_total = 1.0 + strength * (
        centre * sine_square * 0.5 + (upper_line + lower_line) * (1.0 + cosine * cosine) * 0.25
    )
    linear = strength * (centre - 0.5 * (upper_line + lower_line)) * sine_square * 0.5
    linear_cosine = linear * jnp.cos(2.0 * azimuth)
    linear_sine = linear * jnp.sin(2.0 * azimuth)
    circular = strength * (lower_line - upper_line) * cosine * 0.5
    denominator = (
        absorb_total * absorb_total
        - linear_cosine * linear_cosine
        - linear_sine * linear_sine
        - circular * circular
    )
    source_ratio = source_slope / denominator
    return jnp.stack(
        [
            source_zero + source_ratio * absorb_total,
            -source_ratio * linear_cosine,
            -source_ratio * linear_sine,
            -source_ratio * circular,
        ]
    )


def band_tables(tap_table, out_rows, tap_count):
    in_rows = out_rows + tap_count - 1
    target_row = lax.broadcasted_iota(jnp.int32, (out_rows, in_rows, tap_count), 0)
    source_row = lax.broadcasted_iota(jnp.int32, (out_rows, in_rows, tap_count), 1)
    tap_index = lax.broadcasted_iota(jnp.int32, (out_rows, in_rows, tap_count), 2)
    selector = (source_row - target_row == tap_index).astype(jnp.bfloat16)
    return jnp.einsum(
        "wkt,ijt->wkij", tap_table, selector, preferred_element_type=jnp.float32
    ).astype(jnp.bfloat16)


def column_tables(tap_table, columns, tap_count):
    radius = tap_count // 2
    source_column = lax.broadcasted_iota(jnp.int32, (columns, columns, tap_count), 0)
    target_column = lax.broadcasted_iota(jnp.int32, (columns, columns, tap_count), 1)
    tap_index = lax.broadcasted_iota(jnp.int32, (columns, columns, tap_count), 2)
    selector = (source_column - target_column + radius == tap_index).astype(jnp.bfloat16)
    return jnp.einsum(
        "wkt,xyt->wkxy", tap_table, selector, preferred_element_type=jnp.float32
    ).astype(jnp.bfloat16)


def extend(upper_rim, middle, lower_rim, length, axis_index):
    radius = upper_rim.shape[axis_index]
    widened = jnp.concatenate([upper_rim, middle, jnp.zeros_like(upper_rim)], axis=axis_index)
    return lax.dynamic_update_slice_in_dim(widened, lower_rim, radius + length, axis_index)


def per_device(unit_params, observed, psf_rows, psf_cols, pixel_mask, strip_lengths):
    stokes_count, wave_count, capacity, columns = observed.shape
    tap_count = psf_rows.shape[2]
    radius = tap_count // 2
    wave_total = lax.axis_size("wave")
    gathered = gather_by_doubling(unit_params.reshape(1, -1), "wave")
    own_params = (
        gathered.reshape(wave_total, unit_params.shape[0], capacity // wave_total, columns)
        .transpose(1, 0, 2, 3)
        .reshape(unit_params.shape[0], capacity, columns)
    )
    length = strip_lengths[0]
    wave_pos = lax.axis_index("wave")
    levels = (wave_pos * wave_count + jnp.arange(wave_count, dtype=jnp.int32)).astype(jnp.float32)
    wave_grid = -3.0 + 6.0 * levels / (wave_count * lax.axis_size("wave") - 1)
    row_index = jnp.arange(capacity, dtype=jnp.int32)
    rows_live = (row_index < length).astype(jnp.float32)
    model_own = (stokes_model(own_params, wave_grid) * rows_live[:, None]).astype(jnp.bfloat16)
    tail_rows = lax.dynamic_slice_in_dim(model_own, length - radius, radius, 2)
    upper_rim = passed_along(tail_rows, "strip", 1)
    lower_rim = passed_along(model_own[:, :, :radius], "strip", -1)
    model_wide = extend(upper_rim, model_own, lower_rim, length, 2)
    row_band = band_tables(psf_rows, capacity, tap_count)
    column_band = column_tables(psf_cols, columns, tap_count)
    live_mask = pixel_mask.astype(jnp.float32) * rows_live[:, None]
    weight_square = jnp.array(stokes_weight, jnp.float32)
    weight_square = weight_square * weight_square
    block_size = 4
    block_count = wave_count // block_size

    def forward(number, residual_all):
        first_wave = number * block_size
        model_block = lax.dynamic_slice_in_dim(model_wide, first_wave, block_size, 1)
        band_block = lax.dynamic_slice_in_dim(row_band, first_wave, block_size, 0)
        column_block = lax.dynamic_slice_in_dim(column_band, first_wave, block_size, 0)
        observed_block = lax.dynamic_slice_in_dim(observed, first_wave, block_size, 1)
        row_pass = jnp.einsum(
            "wkij,swjc->kswic", band_block, model_block, preferred_element_type=jnp.float32
        ).astype(jnp.bfloat16)
        blurred = jnp.einsum(
            "kswic,wkcd->swid", row_pass, column_block, preferred_element_type=jnp.float32
        )
        residual = (
            loss_scale
            * weight_square[:, None, None, None]
            * live_mask
            * (blurred - observed_block.astype(jnp.float32))
        ).astype(jnp.bfloat16)
        return lax.dynamic_update_slice_in_dim(residual_all, residual, first_wave, 1)

    residual_all = lax.fori_loop(0, block_count, forward, jnp.zeros(observed.shape, jnp.bfloat16))
    row_back = band_tables(psf_rows[:, :, ::-1], capacity, tap_count)
    tail_residual = lax.dynamic_slice_in_dim(residual_all, length - radius, radius, 2)
    upper_resid = passed_along(tail_residual, "strip", 1)
    lower_resid = passed_along(residual_all[:, :, :radius], "strip", -1)
    residual_wide = extend(upper_resid, residual_all, lower_resid, length, 2)

    def backward(number, gradient_sum):
        first_wave = number * block_size
        residual_block = lax.dynamic_slice_in_dim(residual_wide, first_wave, block_size, 1)
        column_block = lax.dynamic_slice_in_dim(column_band, first_wave, block_size, 0)
        back_block = lax.dynamic_slice_in_dim(row_back, first_wave, block_size, 0)
        grid_block = lax.dynamic_slice_in_dim(wave_grid, first_wave, block_size, 0)
        across = jnp.einsum(
            "swjc,wkdc->kswjd", residual_block, column_block, preferred_element_type=jnp.float32
        ).astype(jnp.bfloat16)
        adjoint = (
            jnp.einsum("wkij,kswjc->swic", back_block, across, preferred_element_type=jnp.float32)
            * rows_live[:, None]
        )

        def model_of(params_now):
            return stokes_model(params_now, grid_block)

        unused_model, pullback = jax.vjp(model_of, own_params)
        return gradient_sum + pullback(adjoint)[0]

    gradient_local = lax.fori_loop(
        0, block_count, backward, jnp.zeros(own_params.shape, jnp.float32)
    )
    pieces = gradient_local.reshape(
        gradient_local.shape[0], wave_total, capacity // wave_total, columns
    ).transpose(1, 0, 2, 3)
    return scatter_by_halving(pieces, "wave").reshape(unit_params.shape)


def solution(mesh):
    return jax.shard_map(
        per_device,
        mesh=mesh,
        in_specs=(
            P(None, "strip", "wave"),
            P(None, "wave", "strip", None),
            P("wave", None, None),
            P("wave", None, None),
            P("strip", None),
            P("strip"),
        ),
        out_specs=P(None, "strip", "wave"),
        check_vma=False,
    )
```

```python
import jax
import jax.numpy as jnp
from jax import lax
from jax.sharding import PartitionSpec as P

parameter_low = (0.2, 0.4, 2.0, -0.8, 0.4, 0.3, 0.0, 0.0, 0.0)
parameter_span = (0.4, 0.6, 18.0, 1.6, 0.8, 1.2, 1.5, 3.141592653589793, 3.141592653589793)
stokes_weight = (1.0, 3.0, 3.0, 2.0)
loss_scale = 0.03125


def passed_along(shard, axis, by):
    count = lax.axis_size(axis)
    pairs = [(i, i + by) for i in range(count) if 0 <= i + by < count]
    return lax.ppermute(shard, axis, pairs)


def exchange(shard, axis, bit):
    count = lax.axis_size(axis)
    pairs = [(i, i ^ bit) for i in range(count)]
    return lax.ppermute(shard, axis, pairs)


def gather_by_doubling(shard, axis):
    count = lax.axis_size(axis)
    position = lax.axis_index(axis)
    bit = 1
    while bit < count:
        other = exchange(shard, axis, bit)
        low_side = (position & bit) == 0
        shard = jnp.where(
            low_side,
            jnp.concatenate([shard, other], axis=0),
            jnp.concatenate([other, shard], axis=0),
        )
        bit *= 2
    return shard


def scatter_by_halving(pieces, axis):
    count = lax.axis_size(axis)
    position = lax.axis_index(axis)
    bit = count // 2
    while bit >= 1:
        half = pieces.shape[0] // 2
        high_side = ((position & bit) != 0).astype(jnp.int32)
        keep = lax.dynamic_slice_in_dim(pieces, high_side * half, half, 0)
        give = lax.dynamic_slice_in_dim(pieces, (1 - high_side) * half, half, 0)
        pieces = keep + exchange(give, axis, bit)
        bit //= 2
    return pieces[0]


def profile(distance, damping):
    scaled = distance / damping
    return 1.0 / (1.0 + scaled * scaled)


def stokes_model(unit_params, wave_grid):
    physical = [
        parameter_low[number] + parameter_span[number] * unit_params[number] for number in range(9)
    ]
    (
        source_zero,
        source_slope,
        strength,
        doppler,
        line_width,
        damping,
        zeeman_split,
        incline,
        azimuth,
    ) = physical
    offset = (wave_grid[:, None, None] - doppler) / line_width
    split_ratio = zeeman_split / line_width
    centre = profile(offset, damping)
    upper_line = profile(offset - split_ratio, damping)
    lower_line = profile(offset + split_ratio, damping)
    cosine = jnp.cos(incline)
    sine_value = jnp.sin(incline)
    sine_square = sine_value * sine_value
    absorb_total = 1.0 + strength * (
        centre * sine_square * 0.5 + (upper_line + lower_line) * (1.0 + cosine * cosine) * 0.25
    )
    linear = strength * (centre - 0.5 * (upper_line + lower_line)) * sine_square * 0.5
    linear_cosine = linear * jnp.cos(2.0 * azimuth)
    linear_sine = linear * jnp.sin(2.0 * azimuth)
    circular = strength * (lower_line - upper_line) * cosine * 0.5
    denominator = (
        absorb_total * absorb_total
        - linear_cosine * linear_cosine
        - linear_sine * linear_sine
        - circular * circular
    )
    source_ratio = source_slope / denominator
    return jnp.stack(
        [
            source_zero + source_ratio * absorb_total,
            -source_ratio * linear_cosine,
            -source_ratio * linear_sine,
            -source_ratio * circular,
        ]
    )


def band_tables(tap_table, out_rows, tap_count):
    in_rows = out_rows + tap_count - 1
    target_row = lax.broadcasted_iota(jnp.int32, (out_rows, in_rows, tap_count), 0)
    source_row = lax.broadcasted_iota(jnp.int32, (out_rows, in_rows, tap_count), 1)
    tap_index = lax.broadcasted_iota(jnp.int32, (out_rows, in_rows, tap_count), 2)
    selector = (source_row - target_row == tap_index).astype(jnp.bfloat16)
    return jnp.einsum(
        "wkt,ijt->wkij", tap_table, selector, preferred_element_type=jnp.float32
    ).astype(jnp.bfloat16)


def column_tables(tap_table, columns, tap_count):
    radius = tap_count // 2
    source_column = lax.broadcasted_iota(jnp.int32, (columns, columns, tap_count), 0)
    target_column = lax.broadcasted_iota(jnp.int32, (columns, columns, tap_count), 1)
    tap_index = lax.broadcasted_iota(jnp.int32, (columns, columns, tap_count), 2)
    selector = (source_column - target_column + radius == tap_index).astype(jnp.bfloat16)
    return jnp.einsum(
        "wkt,xyt->wkxy", tap_table, selector, preferred_element_type=jnp.float32
    ).astype(jnp.bfloat16)


def extend(upper_rim, middle, lower_rim, length, axis_index):
    radius = upper_rim.shape[axis_index]
    extent = middle.shape[axis_index]
    wide = extent + 2 * radius

    def padded(part, before, after):
        widths = [(0, 0)] * part.ndim
        widths[axis_index] = (before, after)
        return jnp.pad(part, widths)

    upper_part = padded(upper_rim, 0, wide - radius)
    middle_part = padded(middle, radius, radius)
    lower_pool = padded(lower_rim, wide, wide)
    lower_part = lax.dynamic_slice_in_dim(lower_pool, wide - radius - length, wide, axis_index)
    return upper_part + middle_part + lower_part


def per_device(unit_params, observed, psf_rows, psf_cols, pixel_mask, strip_lengths):
    stokes_count, wave_count, capacity, columns = observed.shape
    tap_count = psf_rows.shape[2]
    radius = tap_count // 2
    wave_total = lax.axis_size("wave")
    gathered = gather_by_doubling(unit_params.reshape(1, -1), "wave")
    own_params = (
        gathered.reshape(wave_total, unit_params.shape[0], capacity // wave_total, columns)
        .transpose(1, 0, 2, 3)
        .reshape(unit_params.shape[0], capacity, columns)
    )
    length = strip_lengths[0]
    wave_pos = lax.axis_index("wave")
    levels = (wave_pos * wave_count + jnp.arange(wave_count, dtype=jnp.int32)).astype(jnp.float32)
    wave_grid = -3.0 + 6.0 * levels / (wave_count * wave_total - 1)
    row_index = jnp.arange(capacity, dtype=jnp.int32)
    rows_live = (row_index < length).astype(jnp.float32)
    model_own = (stokes_model(own_params, wave_grid) * rows_live[:, None]).astype(jnp.bfloat16)
    tail_rows = lax.dynamic_slice_in_dim(model_own, length - radius, radius, 2)
    upper_rim = passed_along(tail_rows, "strip", 1)
    lower_rim = passed_along(model_own[:, :, :radius], "strip", -1)
    model_wide = extend(upper_rim, model_own, lower_rim, length, 2)
    row_band = band_tables(psf_rows, capacity, tap_count)
    column_band = column_tables(psf_cols, columns, tap_count)
    live_mask = pixel_mask.astype(jnp.float32) * rows_live[:, None]
    weight_square = jnp.array(stokes_weight, jnp.float32)
    weight_square = weight_square * weight_square

    row_pass = jnp.einsum(
        "wkij,swjc->kswic", row_band, model_wide, preferred_element_type=jnp.float32
    ).astype(jnp.bfloat16)
    blurred = jnp.einsum(
        "kswic,wkcd->swid", row_pass, column_band, preferred_element_type=jnp.float32
    )
    residual_all = (
        loss_scale
        * weight_square[:, None, None, None]
        * live_mask
        * (blurred - observed.astype(jnp.float32))
    ).astype(jnp.bfloat16)

    row_back = band_tables(psf_rows[:, :, ::-1], capacity, tap_count)
    tail_residual = lax.dynamic_slice_in_dim(residual_all, length - radius, radius, 2)
    upper_resid = passed_along(tail_residual, "strip", 1)
    lower_resid = passed_along(residual_all[:, :, :radius], "strip", -1)
    residual_wide = extend(upper_resid, residual_all, lower_resid, length, 2)

    across = jnp.einsum(
        "swjc,wkdc->kswjd", residual_wide, column_band, preferred_element_type=jnp.float32
    ).astype(jnp.bfloat16)
    adjoint = (
        jnp.einsum("wkij,kswjc->swic", row_back, across, preferred_element_type=jnp.float32)
        * rows_live[:, None]
    )

    def model_of(params_now):
        return stokes_model(params_now, wave_grid)

    unused_model, pullback = jax.vjp(model_of, own_params)
    gradient_local = pullback(adjoint)[0]
    pieces = gradient_local.reshape(
        gradient_local.shape[0], wave_total, capacity // wave_total, columns
    ).transpose(1, 0, 2, 3)
    return scatter_by_halving(pieces, "wave").reshape(unit_params.shape)


def solution(mesh):
    return jax.shard_map(
        per_device,
        mesh=mesh,
        in_specs=(
            P(None, "strip", "wave"),
            P(None, "wave", "strip", None),
            P("wave", None, None),
            P("wave", None, None),
            P("strip", None),
            P("strip"),
        ),
        out_specs=P(None, "strip", "wave"),
        check_vma=False,
    )
```

```python
import jax
import jax.numpy as jnp
from jax import lax
from jax.sharding import PartitionSpec as P

parameter_low = (0.2, 0.4, 2.0, -0.8, 0.4, 0.3, 0.0, 0.0, 0.0)
parameter_span = (0.4, 0.6, 18.0, 1.6, 0.8, 1.2, 1.5, 3.141592653589793, 3.141592653589793)
stokes_weight = (1.0, 3.0, 3.0, 2.0)
loss_scale = 0.03125


def passed_along(shard, axis, by):
    count = lax.axis_size(axis)
    pairs = [(i, i + by) for i in range(count) if 0 <= i + by < count]
    return lax.ppermute(shard, axis, pairs)


def exchange(shard, axis, bit):
    count = lax.axis_size(axis)
    pairs = [(i, i ^ bit) for i in range(count)]
    return lax.ppermute(shard, axis, pairs)


def gather_by_doubling(shard, axis):
    count = lax.axis_size(axis)
    position = lax.axis_index(axis)
    bit = 1
    while bit < count:
        other = exchange(shard, axis, bit)
        low_side = (position & bit) == 0
        shard = jnp.where(
            low_side,
            jnp.concatenate([shard, other], axis=0),
            jnp.concatenate([other, shard], axis=0),
        )
        bit *= 2
    return shard


def scatter_by_halving(pieces, axis):
    count = lax.axis_size(axis)
    position = lax.axis_index(axis)
    bit = count // 2
    while bit >= 1:
        half = pieces.shape[0] // 2
        high_side = ((position & bit) != 0).astype(jnp.int32)
        keep = lax.dynamic_slice_in_dim(pieces, high_side * half, half, 0)
        give = lax.dynamic_slice_in_dim(pieces, (1 - high_side) * half, half, 0)
        pieces = keep + exchange(give, axis, bit)
        bit //= 2
    return pieces[0]


def profile(distance, damping):
    scaled = distance / damping
    return 1.0 / (1.0 + scaled * scaled)


def stokes_model(unit_params, wave_grid, stack_axis=0):
    physical = [
        parameter_low[number] + parameter_span[number] * unit_params[number] for number in range(9)
    ]
    (
        source_zero,
        source_slope,
        strength,
        doppler,
        line_width,
        damping,
        zeeman_split,
        incline,
        azimuth,
    ) = physical
    offset = (wave_grid[:, None, None] - doppler) / line_width
    split_ratio = zeeman_split / line_width
    centre = profile(offset, damping)
    upper_line = profile(offset - split_ratio, damping)
    lower_line = profile(offset + split_ratio, damping)
    cosine = jnp.cos(incline)
    sine_value = jnp.sin(incline)
    sine_square = sine_value * sine_value
    absorb_total = 1.0 + strength * (
        centre * sine_square * 0.5 + (upper_line + lower_line) * (1.0 + cosine * cosine) * 0.25
    )
    linear = strength * (centre - 0.5 * (upper_line + lower_line)) * sine_square * 0.5
    linear_cosine = linear * jnp.cos(2.0 * azimuth)
    linear_sine = linear * jnp.sin(2.0 * azimuth)
    circular = strength * (lower_line - upper_line) * cosine * 0.5
    denominator = (
        absorb_total * absorb_total
        - linear_cosine * linear_cosine
        - linear_sine * linear_sine
        - circular * circular
    )
    source_ratio = source_slope / denominator
    return jnp.stack(
        [
            source_zero + source_ratio * absorb_total,
            -source_ratio * linear_cosine,
            -source_ratio * linear_sine,
            -source_ratio * circular,
        ],
        axis=stack_axis,
    )


def band_tables(tap_table, out_rows, tap_count):
    in_rows = out_rows + tap_count - 1
    target_row = lax.broadcasted_iota(jnp.int32, (out_rows, in_rows, tap_count), 0)
    source_row = lax.broadcasted_iota(jnp.int32, (out_rows, in_rows, tap_count), 1)
    tap_index = lax.broadcasted_iota(jnp.int32, (out_rows, in_rows, tap_count), 2)
    selector = (source_row - target_row == tap_index).astype(jnp.bfloat16)
    return jnp.einsum(
        "wkt,ijt->kwij", tap_table, selector, preferred_element_type=jnp.float32
    ).astype(jnp.bfloat16)


def column_tables(tap_table, columns, tap_count):
    radius = tap_count // 2
    source_column = lax.broadcasted_iota(jnp.int32, (columns, columns, tap_count), 0)
    target_column = lax.broadcasted_iota(jnp.int32, (columns, columns, tap_count), 1)
    tap_index = lax.broadcasted_iota(jnp.int32, (columns, columns, tap_count), 2)
    selector = (source_column - target_column + radius == tap_index).astype(jnp.bfloat16)
    return jnp.einsum(
        "wkt,xyt->kwxy", tap_table, selector, preferred_element_type=jnp.float32
    ).astype(jnp.bfloat16)


def extend(upper_rim, middle, lower_rim, length, axis_index):
    radius = upper_rim.shape[axis_index]
    extent = middle.shape[axis_index]
    wide = extent + 2 * radius

    def padded(part, before, after):
        widths = [(0, 0)] * part.ndim
        widths[axis_index] = (before, after)
        return jnp.pad(part, widths)

    upper_part = padded(upper_rim, 0, wide - radius)
    middle_part = padded(middle, radius, radius)
    lower_pool = padded(lower_rim, wide, wide)
    lower_part = lax.dynamic_slice_in_dim(lower_pool, wide - radius - length, wide, axis_index)
    return upper_part + middle_part + lower_part


def per_device(unit_params, observed, psf_rows, psf_cols, pixel_mask, strip_lengths):
    stokes_count, wave_count, capacity, columns = observed.shape
    tap_count = psf_rows.shape[2]
    radius = tap_count // 2
    wave_total = lax.axis_size("wave")
    gathered = gather_by_doubling(unit_params.reshape(1, -1), "wave")
    own_params = (
        gathered.reshape(wave_total, unit_params.shape[0], capacity // wave_total, columns)
        .transpose(1, 0, 2, 3)
        .reshape(unit_params.shape[0], capacity, columns)
    )
    length = strip_lengths[0]
    wave_pos = lax.axis_index("wave")
    levels = (wave_pos * wave_count + jnp.arange(wave_count, dtype=jnp.int32)).astype(jnp.float32)
    wave_grid = -3.0 + 6.0 * levels / (wave_count * wave_total - 1)
    row_index = jnp.arange(capacity, dtype=jnp.int32)
    rows_live = (row_index < length).astype(jnp.float32)
    live_rows = rows_live[None, :, None, None]
    model_own = (stokes_model(own_params, wave_grid, 2) * live_rows).astype(jnp.bfloat16)
    tail_rows = lax.dynamic_slice_in_dim(model_own, length - radius, radius, 1)
    upper_rim = passed_along(tail_rows, "strip", 1)
    lower_rim = passed_along(model_own[:, :radius], "strip", -1)
    model_wide = extend(upper_rim, model_own, lower_rim, length, 1)
    wide_rows = model_wide.shape[1]
    row_band = band_tables(psf_rows, capacity, tap_count)
    column_band = column_tables(psf_cols, columns, tap_count)
    live_mask = pixel_mask.astype(jnp.float32) * rows_live[:, None]
    weight_square = jnp.array(stokes_weight, jnp.float32)
    weight_square = weight_square * weight_square
    rank = psf_rows.shape[1]

    model_flat = model_wide.reshape(wave_count, wide_rows, stokes_count * columns)
    blurred = None
    for term in range(rank):
        row_pass = jnp.einsum(
            "wij,wjn->win", row_band[term], model_flat, preferred_element_type=jnp.float32
        ).astype(jnp.bfloat16)
        column_pass = jnp.einsum(
            "wmc,wcd->wmd",
            row_pass.reshape(wave_count, capacity * stokes_count, columns),
            column_band[term],
            preferred_element_type=jnp.float32,
        )
        blurred = column_pass if blurred is None else blurred + column_pass
    blurred = blurred.reshape(wave_count, capacity, stokes_count, columns)
    observed_here = observed.transpose(1, 2, 0, 3).astype(jnp.float32)
    residual_all = (
        loss_scale
        * weight_square[None, None, :, None]
        * live_mask[None, :, None, :]
        * (blurred - observed_here)
    ).astype(jnp.bfloat16)

    row_back = band_tables(psf_rows[:, :, ::-1], capacity, tap_count)
    tail_residual = lax.dynamic_slice_in_dim(residual_all, length - radius, radius, 1)
    upper_resid = passed_along(tail_residual, "strip", 1)
    lower_resid = passed_along(residual_all[:, :radius], "strip", -1)
    residual_wide = extend(upper_resid, residual_all, lower_resid, length, 1)
    residual_flat = residual_wide.reshape(wave_count, wide_rows * stokes_count, columns)

    adjoint = None
    for term in range(rank):
        across = jnp.einsum(
            "wmc,wdc->wmd", residual_flat, column_band[term], preferred_element_type=jnp.float32
        ).astype(jnp.bfloat16)
        back_pass = jnp.einsum(
            "wij,wjn->win",
            row_back[term],
            across.reshape(wave_count, wide_rows, stokes_count * columns),
            preferred_element_type=jnp.float32,
        )
        adjoint = back_pass if adjoint is None else adjoint + back_pass
    adjoint = adjoint.reshape(wave_count, capacity, stokes_count, columns) * live_rows

    def model_of(params_now):
        return stokes_model(params_now, wave_grid, 2)

    unused_model, pullback = jax.vjp(model_of, own_params)
    gradient_local = pullback(adjoint)[0]
    pieces = gradient_local.reshape(
        gradient_local.shape[0], wave_total, capacity // wave_total, columns
    ).transpose(1, 0, 2, 3)
    return scatter_by_halving(pieces, "wave").reshape(unit_params.shape)


def solution(mesh):
    return jax.shard_map(
        per_device,
        mesh=mesh,
        in_specs=(
            P(None, "strip", "wave"),
            P(None, "wave", "strip", None),
            P("wave", None, None),
            P("wave", None, None),
            P("strip", None),
            P("strip"),
        ),
        out_specs=P(None, "strip", "wave"),
        check_vma=False,
    )
```

```python
import jax
import jax.numpy as jnp
from jax import lax
from jax.sharding import PartitionSpec as P

parameter_low = (0.2, 0.4, 2.0, -0.8, 0.4, 0.3, 0.0, 0.0, 0.0)
parameter_span = (0.4, 0.6, 18.0, 1.6, 0.8, 1.2, 1.5, 3.141592653589793, 3.141592653589793)
stokes_weight = (1.0, 3.0, 3.0, 2.0)
loss_scale = 0.03125


def passed_along(shard, axis, by):
    count = lax.axis_size(axis)
    pairs = [(i, i + by) for i in range(count) if 0 <= i + by < count]
    return lax.ppermute(shard, axis, pairs)


def exchange(shard, axis, bit):
    count = lax.axis_size(axis)
    pairs = [(i, i ^ bit) for i in range(count)]
    return lax.ppermute(shard, axis, pairs)


def gather_by_doubling(shard, axis):
    count = lax.axis_size(axis)
    position = lax.axis_index(axis)
    bit = 1
    while bit < count:
        other = exchange(shard, axis, bit)
        low_side = (position & bit) == 0
        shard = jnp.where(
            low_side,
            jnp.concatenate([shard, other], axis=0),
            jnp.concatenate([other, shard], axis=0),
        )
        bit *= 2
    return shard


def scatter_by_halving(pieces, axis):
    count = lax.axis_size(axis)
    position = lax.axis_index(axis)
    bit = count // 2
    while bit >= 1:
        half = pieces.shape[0] // 2
        high_side = ((position & bit) != 0).astype(jnp.int32)
        keep = lax.dynamic_slice_in_dim(pieces, high_side * half, half, 0)
        give = lax.dynamic_slice_in_dim(pieces, (1 - high_side) * half, half, 0)
        pieces = keep + exchange(give, axis, bit)
        bit //= 2
    return pieces[0]


def profile(distance, damping):
    scaled = distance / damping
    return 1.0 / (1.0 + scaled * scaled)


def stokes_model(unit_params, wave_grid):
    physical = [
        parameter_low[number] + parameter_span[number] * unit_params[number] for number in range(9)
    ]
    (
        source_zero,
        source_slope,
        strength,
        doppler,
        line_width,
        damping,
        zeeman_split,
        incline,
        azimuth,
    ) = physical
    offset = (wave_grid[:, None, None] - doppler) / line_width
    split_ratio = zeeman_split / line_width
    centre = profile(offset, damping)
    upper_line = profile(offset - split_ratio, damping)
    lower_line = profile(offset + split_ratio, damping)
    cosine = jnp.cos(incline)
    sine_value = jnp.sin(incline)
    sine_square = sine_value * sine_value
    absorb_total = 1.0 + strength * (
        centre * sine_square * 0.5 + (upper_line + lower_line) * (1.0 + cosine * cosine) * 0.25
    )
    linear = strength * (centre - 0.5 * (upper_line + lower_line)) * sine_square * 0.5
    linear_cosine = linear * jnp.cos(2.0 * azimuth)
    linear_sine = linear * jnp.sin(2.0 * azimuth)
    circular = strength * (lower_line - upper_line) * cosine * 0.5
    denominator = (
        absorb_total * absorb_total
        - linear_cosine * linear_cosine
        - linear_sine * linear_sine
        - circular * circular
    )
    source_ratio = source_slope / denominator
    return jnp.stack(
        [
            source_zero + source_ratio * absorb_total,
            -source_ratio * linear_cosine,
            -source_ratio * linear_sine,
            -source_ratio * circular,
        ]
    )


def band_tables(tap_table, out_rows, tap_count):
    in_rows = out_rows + tap_count - 1
    target_row = lax.broadcasted_iota(jnp.int32, (out_rows, in_rows, tap_count), 0)
    source_row = lax.broadcasted_iota(jnp.int32, (out_rows, in_rows, tap_count), 1)
    tap_index = lax.broadcasted_iota(jnp.int32, (out_rows, in_rows, tap_count), 2)
    selector = (source_row - target_row == tap_index).astype(jnp.bfloat16)
    return jnp.einsum(
        "wkt,ijt->wkij", tap_table, selector, preferred_element_type=jnp.float32
    ).astype(jnp.bfloat16)


def column_tables(tap_table, columns, tap_count):
    radius = tap_count // 2
    source_column = lax.broadcasted_iota(jnp.int32, (columns, columns, tap_count), 0)
    target_column = lax.broadcasted_iota(jnp.int32, (columns, columns, tap_count), 1)
    tap_index = lax.broadcasted_iota(jnp.int32, (columns, columns, tap_count), 2)
    selector = (source_column - target_column + radius == tap_index).astype(jnp.bfloat16)
    return jnp.einsum(
        "wkt,xyt->wkxy", tap_table, selector, preferred_element_type=jnp.float32
    ).astype(jnp.bfloat16)


def extend(upper_rim, middle, lower_rim, length, axis_index):
    radius = upper_rim.shape[axis_index]
    extent = middle.shape[axis_index]
    wide = extent + 2 * radius

    def padded(part, before, after):
        widths = [(0, 0)] * part.ndim
        widths[axis_index] = (before, after)
        return jnp.pad(part, widths)

    upper_part = padded(upper_rim, 0, wide - radius)
    middle_part = padded(middle, radius, radius)
    lower_pool = padded(lower_rim, wide, wide)
    lower_part = lax.dynamic_slice_in_dim(lower_pool, wide - radius - length, wide, axis_index)
    return upper_part + middle_part + lower_part


def per_device(unit_params, observed, psf_rows, psf_cols, pixel_mask, strip_lengths):
    stokes_count, wave_count, capacity, columns = observed.shape
    tap_count = psf_rows.shape[2]
    radius = tap_count // 2
    wave_total = lax.axis_size("wave")
    gathered = gather_by_doubling(unit_params.reshape(1, -1), "wave")
    own_params = (
        gathered.reshape(wave_total, unit_params.shape[0], capacity // wave_total, columns)
        .transpose(1, 0, 2, 3)
        .reshape(unit_params.shape[0], capacity, columns)
    )
    length = strip_lengths[0]
    wave_pos = lax.axis_index("wave")
    levels = (wave_pos * wave_count + jnp.arange(wave_count, dtype=jnp.int32)).astype(jnp.float32)
    wave_grid = -3.0 + 6.0 * levels / (wave_count * wave_total - 1)
    row_index = jnp.arange(capacity, dtype=jnp.int32)
    rows_live = (row_index < length).astype(jnp.float32)
    param_tail = lax.dynamic_slice_in_dim(own_params, length - radius, radius, 1)
    upper_params = passed_along(param_tail, "strip", 1)
    lower_params = passed_along(own_params[:, :radius], "strip", -1)
    strip_pos = lax.axis_index("strip")
    has_upper = strip_pos > 0
    has_lower = strip_pos < lax.axis_size("strip") - 1
    model_own = (stokes_model(own_params, wave_grid) * rows_live[:, None]).astype(jnp.bfloat16)
    upper_rim = jnp.where(has_upper, stokes_model(upper_params, wave_grid), 0.0).astype(jnp.bfloat16)
    lower_rim = jnp.where(has_lower, stokes_model(lower_params, wave_grid), 0.0).astype(jnp.bfloat16)
    model_wide = extend(upper_rim, model_own, lower_rim, length, 2)
    row_band = band_tables(psf_rows, capacity, tap_count)
    column_band = column_tables(psf_cols, columns, tap_count)
    live_mask = pixel_mask.astype(jnp.float32) * rows_live[:, None]
    weight_square = jnp.array(stokes_weight, jnp.float32)
    weight_square = weight_square * weight_square

    row_pass = jnp.einsum(
        "wkij,swjc->kswic", row_band, model_wide, preferred_element_type=jnp.float32
    ).astype(jnp.bfloat16)
    blurred = jnp.einsum(
        "kswic,wkcd->swid", row_pass, column_band, preferred_element_type=jnp.float32
    )
    residual_all = (
        loss_scale
        * weight_square[:, None, None, None]
        * live_mask
        * (blurred - observed.astype(jnp.float32))
    ).astype(jnp.bfloat16)

    row_back = band_tables(psf_rows[:, :, ::-1], capacity, tap_count)
    tail_residual = lax.dynamic_slice_in_dim(residual_all, length - radius, radius, 2)
    upper_resid = passed_along(tail_residual, "strip", 1)
    lower_resid = passed_along(residual_all[:, :, :radius], "strip", -1)

    def across_of(residual_rows):
        return jnp.einsum(
            "swjc,wkdc->kswjd", residual_rows, column_band, preferred_element_type=jnp.float32
        ).astype(jnp.bfloat16)

    across_own = across_of(residual_all)
    across = extend(across_of(upper_resid), across_own, across_of(lower_resid), length, 3)
    adjoint = (
        jnp.einsum("wkij,kswjc->swic", row_back, across, preferred_element_type=jnp.float32)
        * rows_live[:, None]
    )

    def model_of(params_now):
        return stokes_model(params_now, wave_grid)

    unused_model, pullback = jax.vjp(model_of, own_params)
    gradient_local = pullback(adjoint)[0]
    pieces = gradient_local.reshape(
        gradient_local.shape[0], wave_total, capacity // wave_total, columns
    ).transpose(1, 0, 2, 3)
    return scatter_by_halving(pieces, "wave").reshape(unit_params.shape)


def solution(mesh):
    return jax.shard_map(
        per_device,
        mesh=mesh,
        in_specs=(
            P(None, "strip", "wave"),
            P(None, "wave", "strip", None),
            P("wave", None, None),
            P("wave", None, None),
            P("strip", None),
            P("strip"),
        ),
        out_specs=P(None, "strip", "wave"),
        check_vma=False,
    )
```

```python
import jax
import jax.numpy as jnp
from jax import lax
from jax.sharding import PartitionSpec as P

parameter_low = (0.2, 0.4, 2.0, -0.8, 0.4, 0.3, 0.0, 0.0, 0.0)
parameter_span = (0.4, 0.6, 18.0, 1.6, 0.8, 1.2, 1.5, 3.141592653589793, 3.141592653589793)
stokes_weight = (1.0, 3.0, 3.0, 2.0)
loss_scale = 0.03125


def passed_along(shard, axis, by):
    count = lax.axis_size(axis)
    pairs = [(i, i + by) for i in range(count) if 0 <= i + by < count]
    return lax.ppermute(shard, axis, pairs)


def exchange(shard, axis, bit):
    count = lax.axis_size(axis)
    pairs = [(i, i ^ bit) for i in range(count)]
    return lax.ppermute(shard, axis, pairs)


def gather_by_doubling(shard, axis):
    count = lax.axis_size(axis)
    position = lax.axis_index(axis)
    bit = 1
    while bit < count:
        other = exchange(shard, axis, bit)
        low_side = (position & bit) == 0
        shard = jnp.where(
            low_side,
            jnp.concatenate([shard, other], axis=0),
            jnp.concatenate([other, shard], axis=0),
        )
        bit *= 2
    return shard


def scatter_by_halving(pieces, axis):
    count = lax.axis_size(axis)
    position = lax.axis_index(axis)
    bit = count // 2
    while bit >= 1:
        half = pieces.shape[0] // 2
        high_side = ((position & bit) != 0).astype(jnp.int32)
        keep = lax.dynamic_slice_in_dim(pieces, high_side * half, half, 0)
        give = lax.dynamic_slice_in_dim(pieces, (1 - high_side) * half, half, 0)
        pieces = keep + exchange(give, axis, bit)
        bit //= 2
    return pieces[0]


def profile(distance, damping):
    scaled = distance / damping
    return 1.0 / (1.0 + scaled * scaled)


def stokes_model(unit_params, wave_grid):
    physical = [
        parameter_low[number] + parameter_span[number] * unit_params[number] for number in range(9)
    ]
    (
        source_zero,
        source_slope,
        strength,
        doppler,
        line_width,
        damping,
        zeeman_split,
        incline,
        azimuth,
    ) = physical
    offset = (wave_grid[:, None, None] - doppler) / line_width
    split_ratio = zeeman_split / line_width
    centre = profile(offset, damping)
    upper_line = profile(offset - split_ratio, damping)
    lower_line = profile(offset + split_ratio, damping)
    cosine = jnp.cos(incline)
    sine_value = jnp.sin(incline)
    sine_square = sine_value * sine_value
    absorb_total = 1.0 + strength * (
        centre * sine_square * 0.5 + (upper_line + lower_line) * (1.0 + cosine * cosine) * 0.25
    )
    linear = strength * (centre - 0.5 * (upper_line + lower_line)) * sine_square * 0.5
    linear_cosine = linear * jnp.cos(2.0 * azimuth)
    linear_sine = linear * jnp.sin(2.0 * azimuth)
    circular = strength * (lower_line - upper_line) * cosine * 0.5
    denominator = (
        absorb_total * absorb_total
        - linear_cosine * linear_cosine
        - linear_sine * linear_sine
        - circular * circular
    )
    source_ratio = source_slope / denominator
    return jnp.stack(
        [
            source_zero + source_ratio * absorb_total,
            -source_ratio * linear_cosine,
            -source_ratio * linear_sine,
            -source_ratio * circular,
        ]
    )


def band_tables(tap_table, out_rows, tap_count):
    in_rows = out_rows + tap_count - 1
    target_row = lax.broadcasted_iota(jnp.int32, (out_rows, in_rows, tap_count), 0)
    source_row = lax.broadcasted_iota(jnp.int32, (out_rows, in_rows, tap_count), 1)
    tap_index = lax.broadcasted_iota(jnp.int32, (out_rows, in_rows, tap_count), 2)
    selector = (source_row - target_row == tap_index).astype(jnp.bfloat16)
    return jnp.einsum(
        "wkt,ijt->wkij", tap_table, selector, preferred_element_type=jnp.float32
    ).astype(jnp.bfloat16)


def column_tables(tap_table, columns, tap_count):
    radius = tap_count // 2
    source_column = lax.broadcasted_iota(jnp.int32, (columns, columns, tap_count), 0)
    target_column = lax.broadcasted_iota(jnp.int32, (columns, columns, tap_count), 1)
    tap_index = lax.broadcasted_iota(jnp.int32, (columns, columns, tap_count), 2)
    selector = (source_column - target_column + radius == tap_index).astype(jnp.bfloat16)
    return jnp.einsum(
        "wkt,xyt->wkxy", tap_table, selector, preferred_element_type=jnp.float32
    ).astype(jnp.bfloat16)


def extend(upper_rim, middle, lower_rim, length, axis_index):
    radius = upper_rim.shape[axis_index]
    extent = middle.shape[axis_index]
    wide = extent + 2 * radius

    def padded(part, before, after):
        widths = [(0, 0)] * part.ndim
        widths[axis_index] = (before, after)
        return jnp.pad(part, widths)

    upper_part = padded(upper_rim, 0, wide - radius)
    middle_part = padded(middle, radius, radius)
    lower_pool = padded(lower_rim, wide, wide)
    lower_part = lax.dynamic_slice_in_dim(lower_pool, wide - radius - length, wide, axis_index)
    return upper_part + middle_part + lower_part


def per_device(unit_params, observed, psf_rows, psf_cols, pixel_mask, strip_lengths):
    stokes_count, wave_count, capacity, columns = observed.shape
    tap_count = psf_rows.shape[2]
    radius = tap_count // 2
    wave_total = lax.axis_size("wave")
    gathered = gather_by_doubling(unit_params.reshape(1, -1), "wave")
    own_params = (
        gathered.reshape(wave_total, unit_params.shape[0], capacity // wave_total, columns)
        .transpose(1, 0, 2, 3)
        .reshape(unit_params.shape[0], capacity, columns)
    )
    length = strip_lengths[0]
    wave_pos = lax.axis_index("wave")
    levels = (wave_pos * wave_count + jnp.arange(wave_count, dtype=jnp.int32)).astype(jnp.float32)
    wave_grid = -3.0 + 6.0 * levels / (wave_count * wave_total - 1)
    row_index = jnp.arange(capacity, dtype=jnp.int32)
    rows_live = (row_index < length).astype(jnp.float32)
    param_tail = lax.dynamic_slice_in_dim(own_params, length - radius, radius, 1)
    upper_params = passed_along(param_tail, "strip", 1)
    lower_params = passed_along(own_params[:, :radius], "strip", -1)
    strip_pos = lax.axis_index("strip")
    has_upper = strip_pos > 0
    has_lower = strip_pos < lax.axis_size("strip") - 1
    model_own = (stokes_model(own_params, wave_grid) * rows_live[:, None]).astype(jnp.bfloat16)
    upper_rim = jnp.where(has_upper, stokes_model(upper_params, wave_grid), 0.0).astype(jnp.bfloat16)
    lower_rim = jnp.where(has_lower, stokes_model(lower_params, wave_grid), 0.0).astype(jnp.bfloat16)
    model_wide = extend(upper_rim, model_own, lower_rim, length, 2)
    row_band = band_tables(psf_rows, capacity, tap_count)
    column_band = column_tables(psf_cols, columns, tap_count)
    live_mask = pixel_mask.astype(jnp.float32) * rows_live[:, None]
    weight_square = jnp.array(stokes_weight, jnp.float32)
    weight_square = weight_square * weight_square

    row_pass = jnp.einsum(
        "wkij,swjc->kswic", row_band, model_wide, preferred_element_type=jnp.float32
    ).astype(jnp.bfloat16)
    blurred = jnp.einsum(
        "kswic,wkcd->swid", row_pass, column_band, preferred_element_type=jnp.float32
    )
    residual_all = (
        loss_scale
        * weight_square[:, None, None, None]
        * live_mask
        * (blurred - observed.astype(jnp.float32))
    ).astype(jnp.bfloat16)

    row_back = band_tables(psf_rows[:, :, ::-1], capacity, tap_count)
    tail_residual = lax.dynamic_slice_in_dim(residual_all, length - radius, radius, 2)
    upper_resid = passed_along(tail_residual, "strip", 1)
    lower_resid = passed_along(residual_all[:, :, :radius], "strip", -1)
    residual_wide = extend(upper_resid, residual_all, lower_resid, length, 2)

    across = jnp.einsum(
        "swjc,wkdc->kswjd", residual_wide, column_band, preferred_element_type=jnp.float32
    ).astype(jnp.bfloat16)
    adjoint = (
        jnp.einsum("wkij,kswjc->swic", row_back, across, preferred_element_type=jnp.float32)
        * rows_live[:, None]
    )

    def model_of(params_now):
        return stokes_model(params_now, wave_grid)

    unused_model, pullback = jax.vjp(model_of, own_params)
    gradient_local = pullback(adjoint)[0]
    pieces = gradient_local.reshape(
        gradient_local.shape[0], wave_total, capacity // wave_total, columns
    ).transpose(1, 0, 2, 3)
    return scatter_by_halving(pieces, "wave").reshape(unit_params.shape)


def solution(mesh):
    return jax.shard_map(
        per_device,
        mesh=mesh,
        in_specs=(
            P(None, "strip", "wave"),
            P(None, "wave", "strip", None),
            P("wave", None, None),
            P("wave", None, None),
            P("strip", None),
            P("strip"),
        ),
        out_specs=P(None, "strip", "wave"),
        check_vma=False,
    )
```

```python
import jax
import jax.numpy as jnp
from jax import lax
from jax.sharding import PartitionSpec as P

parameter_low = (0.2, 0.4, 2.0, -0.8, 0.4, 0.3, 0.0, 0.0, 0.0)
parameter_span = (0.4, 0.6, 18.0, 1.6, 0.8, 1.2, 1.5, 3.141592653589793, 3.141592653589793)
stokes_weight = (1.0, 3.0, 3.0, 2.0)
loss_scale = 0.03125


def passed_along(shard, axis, by):
    count = lax.axis_size(axis)
    pairs = [(i, i + by) for i in range(count) if 0 <= i + by < count]
    return lax.ppermute(shard, axis, pairs)


def exchange(shard, axis, bit):
    count = lax.axis_size(axis)
    pairs = [(i, i ^ bit) for i in range(count)]
    return lax.ppermute(shard, axis, pairs)


def gather_by_doubling(shard, axis):
    count = lax.axis_size(axis)
    position = lax.axis_index(axis)
    bit = 1
    while bit < count:
        other = exchange(shard, axis, bit)
        low_side = (position & bit) == 0
        shard = jnp.where(
            low_side,
            jnp.concatenate([shard, other], axis=0),
            jnp.concatenate([other, shard], axis=0),
        )
        bit *= 2
    return shard


def scatter_by_halving(pieces, axis):
    count = lax.axis_size(axis)
    position = lax.axis_index(axis)
    bit = count // 2
    while bit >= 1:
        half = pieces.shape[0] // 2
        high_side = ((position & bit) != 0).astype(jnp.int32)
        keep = lax.dynamic_slice_in_dim(pieces, high_side * half, half, 0)
        give = lax.dynamic_slice_in_dim(pieces, (1 - high_side) * half, half, 0)
        pieces = keep + exchange(give, axis, bit)
        bit //= 2
    return pieces[0]


def profile(distance, damping):
    scaled = distance / damping
    return 1.0 / (1.0 + scaled * scaled)


def stokes_model(unit_params, wave_grid):
    physical = [
        parameter_low[number] + parameter_span[number] * unit_params[number] for number in range(9)
    ]
    (
        source_zero,
        source_slope,
        strength,
        doppler,
        line_width,
        damping,
        zeeman_split,
        incline,
        azimuth,
    ) = physical
    offset = (wave_grid[:, None, None] - doppler) / line_width
    split_ratio = zeeman_split / line_width
    centre = profile(offset, damping)
    upper_line = profile(offset - split_ratio, damping)
    lower_line = profile(offset + split_ratio, damping)
    cosine = jnp.cos(incline)
    sine_value = jnp.sin(incline)
    sine_square = sine_value * sine_value
    absorb_total = 1.0 + strength * (
        centre * sine_square * 0.5 + (upper_line + lower_line) * (1.0 + cosine * cosine) * 0.25
    )
    linear = strength * (centre - 0.5 * (upper_line + lower_line)) * sine_square * 0.5
    linear_cosine = linear * jnp.cos(2.0 * azimuth)
    linear_sine = linear * jnp.sin(2.0 * azimuth)
    circular = strength * (lower_line - upper_line) * cosine * 0.5
    denominator = (
        absorb_total * absorb_total
        - linear_cosine * linear_cosine
        - linear_sine * linear_sine
        - circular * circular
    )
    source_ratio = source_slope / denominator
    return jnp.stack(
        [
            source_zero + source_ratio * absorb_total,
            -source_ratio * linear_cosine,
            -source_ratio * linear_sine,
            -source_ratio * circular,
        ]
    )


def band_tables(tap_table, out_rows, tap_count):
    in_rows = out_rows + tap_count - 1
    target_row = lax.broadcasted_iota(jnp.int32, (out_rows, in_rows, tap_count), 0)
    source_row = lax.broadcasted_iota(jnp.int32, (out_rows, in_rows, tap_count), 1)
    tap_index = lax.broadcasted_iota(jnp.int32, (out_rows, in_rows, tap_count), 2)
    selector = (source_row - target_row == tap_index).astype(jnp.bfloat16)
    return jnp.einsum(
        "wkt,ijt->wkij", tap_table, selector, preferred_element_type=jnp.float32
    ).astype(jnp.bfloat16)


def column_tables(tap_table, columns, tap_count):
    radius = tap_count // 2
    source_column = lax.broadcasted_iota(jnp.int32, (columns, columns, tap_count), 0)
    target_column = lax.broadcasted_iota(jnp.int32, (columns, columns, tap_count), 1)
    tap_index = lax.broadcasted_iota(jnp.int32, (columns, columns, tap_count), 2)
    selector = (source_column - target_column + radius == tap_index).astype(jnp.bfloat16)
    return jnp.einsum(
        "wkt,xyt->wkxy", tap_table, selector, preferred_element_type=jnp.float32
    ).astype(jnp.bfloat16)


def extend(upper_rim, middle, lower_rim, length, axis_index):
    radius = upper_rim.shape[axis_index]
    extent = middle.shape[axis_index]
    wide = extent + 2 * radius

    def padded(part, before, after):
        widths = [(0, 0)] * part.ndim
        widths[axis_index] = (before, after)
        return jnp.pad(part, widths)

    upper_part = padded(upper_rim, 0, wide - radius)
    middle_part = padded(middle, radius, radius)
    lower_pool = padded(lower_rim, wide, wide)
    lower_part = lax.dynamic_slice_in_dim(lower_pool, wide - radius - length, wide, axis_index)
    return upper_part + middle_part + lower_part


def per_device(unit_params, observed, psf_rows, psf_cols, pixel_mask, strip_lengths):
    stokes_count, wave_count, capacity, columns = observed.shape
    tap_count = psf_rows.shape[2]
    radius = tap_count // 2
    wave_total = lax.axis_size("wave")
    gathered = gather_by_doubling(unit_params.reshape(1, -1), "wave")
    own_params = (
        gathered.reshape(wave_total, unit_params.shape[0], capacity // wave_total, columns)
        .transpose(1, 0, 2, 3)
        .reshape(unit_params.shape[0], capacity, columns)
    )
    length = strip_lengths[0]
    wave_pos = lax.axis_index("wave")
    levels = (wave_pos * wave_count + jnp.arange(wave_count, dtype=jnp.int32)).astype(jnp.float32)
    wave_grid = -3.0 + 6.0 * levels / (wave_count * wave_total - 1)
    row_index = jnp.arange(capacity, dtype=jnp.int32)
    rows_live = (row_index < length).astype(jnp.float32)
    param_tail = lax.dynamic_slice_in_dim(own_params, length - radius, radius, 1)
    upper_params = passed_along(param_tail, "strip", 1)
    lower_params = passed_along(own_params[:, :radius], "strip", -1)
    strip_pos = lax.axis_index("strip")
    has_upper = strip_pos > 0
    has_lower = strip_pos < lax.axis_size("strip") - 1
    model_own = (stokes_model(own_params, wave_grid) * rows_live[:, None]).astype(jnp.bfloat16)
    upper_rim = jnp.where(has_upper, stokes_model(upper_params, wave_grid), 0.0).astype(jnp.bfloat16)
    lower_rim = jnp.where(has_lower, stokes_model(lower_params, wave_grid), 0.0).astype(jnp.bfloat16)
    model_wide = extend(upper_rim, model_own, lower_rim, length, 2)
    row_band = band_tables(psf_rows, capacity, tap_count)
    column_band = column_tables(psf_cols, columns, tap_count)
    live_mask = pixel_mask.astype(jnp.float32) * rows_live[:, None]
    weight_square = jnp.array(stokes_weight, jnp.float32)
    weight_square = weight_square * weight_square

    row_pass = jnp.einsum(
        "wkij,swjc->kswic", row_band, model_wide, preferred_element_type=jnp.float32
    ).astype(jnp.bfloat16)
    blurred = jnp.einsum(
        "kswic,wkcd->swid", row_pass, column_band, preferred_element_type=jnp.float32
    )
    residual_all = (
        loss_scale
        * weight_square[:, None, None, None]
        * live_mask
        * (blurred - observed.astype(jnp.float32))
    ).astype(jnp.bfloat16)

    row_back = band_tables(psf_rows[:, :, ::-1], capacity, tap_count)
    tail_residual = lax.dynamic_slice_in_dim(residual_all, length - radius, radius, 2)
    upper_resid = passed_along(tail_residual, "strip", 1)
    lower_resid = passed_along(residual_all[:, :, :radius], "strip", -1)
    def model_of(params_now):
        return stokes_model(params_now, wave_grid)

    unused_model, pullback = jax.vjp(model_of, own_params)
    saved, saved_tree = jax.tree_util.tree_flatten(pullback)
    saved, upper_resid, lower_resid = lax.optimization_barrier((saved, upper_resid, lower_resid))
    pullback = jax.tree_util.tree_unflatten(saved_tree, saved)
    residual_wide = extend(upper_resid, residual_all, lower_resid, length, 2)

    across = jnp.einsum(
        "swjc,wkdc->kswjd", residual_wide, column_band, preferred_element_type=jnp.float32
    ).astype(jnp.bfloat16)
    adjoint = (
        jnp.einsum("wkij,kswjc->swic", row_back, across, preferred_element_type=jnp.float32)
        * rows_live[:, None]
    )

    gradient_local = pullback(adjoint)[0]
    pieces = gradient_local.reshape(
        gradient_local.shape[0], wave_total, capacity // wave_total, columns
    ).transpose(1, 0, 2, 3)
    return scatter_by_halving(pieces, "wave").reshape(unit_params.shape)


def solution(mesh):
    return jax.shard_map(
        per_device,
        mesh=mesh,
        in_specs=(
            P(None, "strip", "wave"),
            P(None, "wave", "strip", None),
            P("wave", None, None),
            P("wave", None, None),
            P("strip", None),
            P("strip"),
        ),
        out_specs=P(None, "strip", "wave"),
        check_vma=False,
    )
```

```python
import jax
import jax.numpy as jnp
from jax import lax
from jax.sharding import PartitionSpec as P

parameter_low = (0.2, 0.4, 2.0, -0.8, 0.4, 0.3, 0.0, 0.0, 0.0)
parameter_span = (0.4, 0.6, 18.0, 1.6, 0.8, 1.2, 1.5, 3.141592653589793, 3.141592653589793)
stokes_weight = (1.0, 3.0, 3.0, 2.0)
loss_scale = 0.03125


def passed_along(shard, axis, by):
    count = lax.axis_size(axis)
    pairs = [(i, i + by) for i in range(count) if 0 <= i + by < count]
    return lax.ppermute(shard, axis, pairs)


def exchange(shard, axis, bit):
    count = lax.axis_size(axis)
    pairs = [(i, i ^ bit) for i in range(count)]
    return lax.ppermute(shard, axis, pairs)


def gather_by_doubling(shard, axis):
    count = lax.axis_size(axis)
    position = lax.axis_index(axis)
    bit = 1
    while bit < count:
        other = exchange(shard, axis, bit)
        low_side = (position & bit) == 0
        shard = jnp.where(
            low_side,
            jnp.concatenate([shard, other], axis=0),
            jnp.concatenate([other, shard], axis=0),
        )
        bit *= 2
    return shard


def scatter_by_halving(pieces, axis):
    count = lax.axis_size(axis)
    position = lax.axis_index(axis)
    bit = count // 2
    while bit >= 1:
        half = pieces.shape[0] // 2
        high_side = ((position & bit) != 0).astype(jnp.int32)
        keep = lax.dynamic_slice_in_dim(pieces, high_side * half, half, 0)
        give = lax.dynamic_slice_in_dim(pieces, (1 - high_side) * half, half, 0)
        pieces = keep + exchange(give, axis, bit)
        bit //= 2
    return pieces[0]


def profile(distance, damping):
    scaled = distance / damping
    return 1.0 / (1.0 + scaled * scaled)


def stokes_model(unit_params, wave_grid):
    physical = [
        parameter_low[number] + parameter_span[number] * unit_params[number] for number in range(9)
    ]
    (
        source_zero,
        source_slope,
        strength,
        doppler,
        line_width,
        damping,
        zeeman_split,
        incline,
        azimuth,
    ) = physical
    offset = (wave_grid[:, None, None] - doppler) / line_width
    split_ratio = zeeman_split / line_width
    centre = profile(offset, damping)
    upper_line = profile(offset - split_ratio, damping)
    lower_line = profile(offset + split_ratio, damping)
    cosine = jnp.cos(incline)
    sine_value = jnp.sin(incline)
    sine_square = sine_value * sine_value
    absorb_total = 1.0 + strength * (
        centre * sine_square * 0.5 + (upper_line + lower_line) * (1.0 + cosine * cosine) * 0.25
    )
    linear = strength * (centre - 0.5 * (upper_line + lower_line)) * sine_square * 0.5
    linear_cosine = linear * jnp.cos(2.0 * azimuth)
    linear_sine = linear * jnp.sin(2.0 * azimuth)
    circular = strength * (lower_line - upper_line) * cosine * 0.5
    denominator = (
        absorb_total * absorb_total
        - linear_cosine * linear_cosine
        - linear_sine * linear_sine
        - circular * circular
    )
    source_ratio = source_slope / denominator
    return jnp.stack(
        [
            source_zero + source_ratio * absorb_total,
            -source_ratio * linear_cosine,
            -source_ratio * linear_sine,
            -source_ratio * circular,
        ]
    )


def band_tables(tap_table, out_rows, tap_count):
    in_rows = out_rows + tap_count - 1
    target_row = lax.broadcasted_iota(jnp.int32, (out_rows, in_rows, tap_count), 0)
    source_row = lax.broadcasted_iota(jnp.int32, (out_rows, in_rows, tap_count), 1)
    tap_index = lax.broadcasted_iota(jnp.int32, (out_rows, in_rows, tap_count), 2)
    selector = (source_row - target_row == tap_index).astype(jnp.bfloat16)
    return jnp.einsum(
        "wkt,ijt->wkij", tap_table, selector, preferred_element_type=jnp.float32
    ).astype(jnp.bfloat16)


def column_tables(tap_table, columns, tap_count):
    radius = tap_count // 2
    source_column = lax.broadcasted_iota(jnp.int32, (columns, columns, tap_count), 0)
    target_column = lax.broadcasted_iota(jnp.int32, (columns, columns, tap_count), 1)
    tap_index = lax.broadcasted_iota(jnp.int32, (columns, columns, tap_count), 2)
    selector = (source_column - target_column + radius == tap_index).astype(jnp.bfloat16)
    return jnp.einsum(
        "wkt,xyt->wkxy", tap_table, selector, preferred_element_type=jnp.float32
    ).astype(jnp.bfloat16)


def extend(upper_rim, middle, lower_rim, length, axis_index):
    radius = upper_rim.shape[axis_index]
    extent = middle.shape[axis_index]
    wide = extent + 2 * radius

    def padded(part, before, after):
        widths = [(0, 0)] * part.ndim
        widths[axis_index] = (before, after)
        return jnp.pad(part, widths)

    upper_part = padded(upper_rim, 0, wide - radius)
    middle_part = padded(middle, radius, radius)
    lower_pool = padded(lower_rim, wide, wide)
    lower_part = lax.dynamic_slice_in_dim(lower_pool, wide - radius - length, wide, axis_index)
    return upper_part + middle_part + lower_part


def per_device(unit_params, observed, psf_rows, psf_cols, pixel_mask, strip_lengths):
    stokes_count, wave_count, capacity, columns = observed.shape
    tap_count = psf_rows.shape[2]
    radius = tap_count // 2
    wave_total = lax.axis_size("wave")
    gathered = gather_by_doubling(unit_params.reshape(1, -1), "wave")
    own_params = (
        gathered.reshape(wave_total, unit_params.shape[0], capacity // wave_total, columns)
        .transpose(1, 0, 2, 3)
        .reshape(unit_params.shape[0], capacity, columns)
    )
    length = strip_lengths[0]
    wave_pos = lax.axis_index("wave")
    levels = (wave_pos * wave_count + jnp.arange(wave_count, dtype=jnp.int32)).astype(jnp.float32)
    wave_grid = -3.0 + 6.0 * levels / (wave_count * wave_total - 1)
    row_index = jnp.arange(capacity, dtype=jnp.int32)
    rows_live = (row_index < length).astype(jnp.float32)
    param_tail = lax.dynamic_slice_in_dim(own_params, length - radius, radius, 1)
    upper_params = passed_along(param_tail, "strip", 1)
    lower_params = passed_along(own_params[:, :radius], "strip", -1)
    strip_pos = lax.axis_index("strip")
    has_upper = strip_pos > 0
    has_lower = strip_pos < lax.axis_size("strip") - 1
    row_band = band_tables(psf_rows, capacity, tap_count)
    column_band = column_tables(psf_cols, columns, tap_count)
    row_back = band_tables(psf_rows[:, :, ::-1], capacity, tap_count)
    live_mask = pixel_mask.astype(jnp.float32) * rows_live[:, None]
    weight_square = jnp.array(stokes_weight, jnp.float32)
    weight_square = weight_square * weight_square
    group_count = 2
    group_width = wave_count // group_count
    residual_groups = []
    for group in range(group_count):
        waves = slice(group * group_width, (group + 1) * group_width)
        grid_part = wave_grid[waves]
        model_own = (stokes_model(own_params, grid_part) * rows_live[:, None]).astype(jnp.bfloat16)
        upper_rim = jnp.where(has_upper, stokes_model(upper_params, grid_part), 0.0)
        lower_rim = jnp.where(has_lower, stokes_model(lower_params, grid_part), 0.0)
        model_wide = extend(
            upper_rim.astype(jnp.bfloat16), model_own, lower_rim.astype(jnp.bfloat16), length, 2
        )
        row_pass = jnp.einsum(
            "wkij,swjc->kswic", row_band[waves], model_wide, preferred_element_type=jnp.float32
        ).astype(jnp.bfloat16)
        blurred = jnp.einsum(
            "kswic,wkcd->swid", row_pass, column_band[waves], preferred_element_type=jnp.float32
        )
        residual_all = (
            loss_scale
            * weight_square[:, None, None, None]
            * live_mask
            * (blurred - observed[:, waves].astype(jnp.float32))
        ).astype(jnp.bfloat16)
        tail_residual = lax.dynamic_slice_in_dim(residual_all, length - radius, radius, 2)
        upper_resid = passed_along(tail_residual, "strip", 1)
        lower_resid = passed_along(residual_all[:, :, :radius], "strip", -1)
        residual_groups.append((residual_all, upper_resid, lower_resid))

    gradient_local = None
    for group in range(group_count):
        waves = slice(group * group_width, (group + 1) * group_width)
        grid_part = wave_grid[waves]
        residual_all, upper_resid, lower_resid = residual_groups[group]
        residual_wide = extend(upper_resid, residual_all, lower_resid, length, 2)
        across = jnp.einsum(
            "swjc,wkdc->kswjd", residual_wide, column_band[waves], preferred_element_type=jnp.float32
        ).astype(jnp.bfloat16)
        adjoint = (
            jnp.einsum("wkij,kswjc->swic", row_back[waves], across, preferred_element_type=jnp.float32)
            * rows_live[:, None]
        )

        def model_of(params_now):
            return stokes_model(params_now, grid_part)

        unused_model, pullback = jax.vjp(model_of, own_params)
        gradient_part = pullback(adjoint)[0]
        gradient_local = gradient_part if gradient_local is None else gradient_local + gradient_part
    pieces = gradient_local.reshape(
        gradient_local.shape[0], wave_total, capacity // wave_total, columns
    ).transpose(1, 0, 2, 3)
    return scatter_by_halving(pieces, "wave").reshape(unit_params.shape)


def solution(mesh):
    return jax.shard_map(
        per_device,
        mesh=mesh,
        in_specs=(
            P(None, "strip", "wave"),
            P(None, "wave", "strip", None),
            P("wave", None, None),
            P("wave", None, None),
            P("strip", None),
            P("strip"),
        ),
        out_specs=P(None, "strip", "wave"),
        check_vma=False,
    )
```

```python
import jax
import jax.numpy as jnp
from jax import lax
from jax.sharding import PartitionSpec as P

parameter_low = (0.2, 0.4, 2.0, -0.8, 0.4, 0.3, 0.0, 0.0, 0.0)
parameter_span = (0.4, 0.6, 18.0, 1.6, 0.8, 1.2, 1.5, 3.141592653589793, 3.141592653589793)
stokes_weight = (1.0, 3.0, 3.0, 2.0)
loss_scale = 0.03125


def passed_along(shard, axis, by):
    count = lax.axis_size(axis)
    pairs = [(i, i + by) for i in range(count) if 0 <= i + by < count]
    return lax.ppermute(shard, axis, pairs)


def exchange(shard, axis, bit):
    count = lax.axis_size(axis)
    pairs = [(i, i ^ bit) for i in range(count)]
    return lax.ppermute(shard, axis, pairs)


def gather_by_doubling(shard, axis):
    count = lax.axis_size(axis)
    position = lax.axis_index(axis)
    bit = 1
    while bit < count:
        other = exchange(shard, axis, bit)
        low_side = (position & bit) == 0
        shard = jnp.where(
            low_side,
            jnp.concatenate([shard, other], axis=0),
            jnp.concatenate([other, shard], axis=0),
        )
        bit *= 2
    return shard


def scatter_by_halving(pieces, axis, bit):
    position = lax.axis_index(axis)
    while bit >= 1:
        half = pieces.shape[0] // 2
        high_side = ((position & bit) != 0).astype(jnp.int32)
        keep = lax.dynamic_slice_in_dim(pieces, high_side * half, half, 0)
        give = lax.dynamic_slice_in_dim(pieces, (1 - high_side) * half, half, 0)
        pieces = keep + exchange(give, axis, bit)
        bit //= 2
    return pieces[0]


def profile(distance, damping):
    scaled = distance / damping
    return 1.0 / (1.0 + scaled * scaled)


def stokes_model(unit_params, wave_grid):
    physical = [
        parameter_low[number] + parameter_span[number] * unit_params[number] for number in range(9)
    ]
    (
        source_zero,
        source_slope,
        strength,
        doppler,
        line_width,
        damping,
        zeeman_split,
        incline,
        azimuth,
    ) = physical
    offset = (wave_grid[:, None, None] - doppler) / line_width
    split_ratio = zeeman_split / line_width
    centre = profile(offset, damping)
    upper_line = profile(offset - split_ratio, damping)
    lower_line = profile(offset + split_ratio, damping)
    cosine = jnp.cos(incline)
    sine_value = jnp.sin(incline)
    sine_square = sine_value * sine_value
    absorb_total = 1.0 + strength * (
        centre * sine_square * 0.5 + (upper_line + lower_line) * (1.0 + cosine * cosine) * 0.25
    )
    linear = strength * (centre - 0.5 * (upper_line + lower_line)) * sine_square * 0.5
    linear_cosine = linear * jnp.cos(2.0 * azimuth)
    linear_sine = linear * jnp.sin(2.0 * azimuth)
    circular = strength * (lower_line - upper_line) * cosine * 0.5
    denominator = (
        absorb_total * absorb_total
        - linear_cosine * linear_cosine
        - linear_sine * linear_sine
        - circular * circular
    )
    source_ratio = source_slope / denominator
    return jnp.stack(
        [
            source_zero + source_ratio * absorb_total,
            -source_ratio * linear_cosine,
            -source_ratio * linear_sine,
            -source_ratio * circular,
        ]
    )


def band_tables(tap_table, out_rows, tap_count):
    in_rows = out_rows + tap_count - 1
    target_row = lax.broadcasted_iota(jnp.int32, (out_rows, in_rows, tap_count), 0)
    source_row = lax.broadcasted_iota(jnp.int32, (out_rows, in_rows, tap_count), 1)
    tap_index = lax.broadcasted_iota(jnp.int32, (out_rows, in_rows, tap_count), 2)
    selector = (source_row - target_row == tap_index).astype(jnp.bfloat16)
    return jnp.einsum(
        "wkt,ijt->wkij", tap_table, selector, preferred_element_type=jnp.float32
    ).astype(jnp.bfloat16)


def column_tables(tap_table, columns, tap_count):
    radius = tap_count // 2
    source_column = lax.broadcasted_iota(jnp.int32, (columns, columns, tap_count), 0)
    target_column = lax.broadcasted_iota(jnp.int32, (columns, columns, tap_count), 1)
    tap_index = lax.broadcasted_iota(jnp.int32, (columns, columns, tap_count), 2)
    selector = (source_column - target_column + radius == tap_index).astype(jnp.bfloat16)
    return jnp.einsum(
        "wkt,xyt->wkxy", tap_table, selector, preferred_element_type=jnp.float32
    ).astype(jnp.bfloat16)


def extend(upper_rim, middle, lower_rim, length, axis_index):
    radius = upper_rim.shape[axis_index]
    extent = middle.shape[axis_index]
    wide = extent + 2 * radius

    def padded(part, before, after):
        widths = [(0, 0)] * part.ndim
        widths[axis_index] = (before, after)
        return jnp.pad(part, widths)

    upper_part = padded(upper_rim, 0, wide - radius)
    middle_part = padded(middle, radius, radius)
    lower_pool = padded(lower_rim, wide, wide)
    lower_part = lax.dynamic_slice_in_dim(lower_pool, wide - radius - length, wide, axis_index)
    return upper_part + middle_part + lower_part


def per_device(unit_params, observed, psf_rows, psf_cols, pixel_mask, strip_lengths):
    stokes_count, wave_count, capacity, columns = observed.shape
    tap_count = psf_rows.shape[2]
    radius = tap_count // 2
    wave_total = lax.axis_size("wave")
    gathered = gather_by_doubling(unit_params.reshape(1, -1), "wave")
    own_params = (
        gathered.reshape(wave_total, unit_params.shape[0], capacity // wave_total, columns)
        .transpose(1, 0, 2, 3)
        .reshape(unit_params.shape[0], capacity, columns)
    )
    length = strip_lengths[0]
    wave_pos = lax.axis_index("wave")
    levels = (wave_pos * wave_count + jnp.arange(wave_count, dtype=jnp.int32)).astype(jnp.float32)
    wave_grid = -3.0 + 6.0 * levels / (wave_count * wave_total - 1)
    row_index = jnp.arange(capacity, dtype=jnp.int32)
    rows_live = (row_index < length).astype(jnp.float32)
    param_tail = lax.dynamic_slice_in_dim(own_params, length - radius, radius, 1)
    upper_params = passed_along(param_tail, "strip", 1)
    lower_params = passed_along(own_params[:, :radius], "strip", -1)
    strip_pos = lax.axis_index("strip")
    has_upper = strip_pos > 0
    has_lower = strip_pos < lax.axis_size("strip") - 1
    model_own = (stokes_model(own_params, wave_grid) * rows_live[:, None]).astype(jnp.bfloat16)
    upper_rim = jnp.where(has_upper, stokes_model(upper_params, wave_grid), 0.0).astype(jnp.bfloat16)
    lower_rim = jnp.where(has_lower, stokes_model(lower_params, wave_grid), 0.0).astype(jnp.bfloat16)
    model_wide = extend(upper_rim, model_own, lower_rim, length, 2)
    row_band = band_tables(psf_rows, capacity, tap_count)
    column_band = column_tables(psf_cols, columns, tap_count)
    live_mask = pixel_mask.astype(jnp.float32) * rows_live[:, None]
    weight_square = jnp.array(stokes_weight, jnp.float32)
    weight_square = weight_square * weight_square

    row_pass = jnp.einsum(
        "wkij,swjc->kswic", row_band, model_wide, preferred_element_type=jnp.float32
    ).astype(jnp.bfloat16)
    blurred = jnp.einsum(
        "kswic,wkcd->swid", row_pass, column_band, preferred_element_type=jnp.float32
    )
    residual_all = (
        loss_scale
        * weight_square[:, None, None, None]
        * live_mask
        * (blurred - observed.astype(jnp.float32))
    ).astype(jnp.bfloat16)

    row_back = band_tables(psf_rows[:, :, ::-1], capacity, tap_count)
    tail_residual = lax.dynamic_slice_in_dim(residual_all, length - radius, radius, 2)
    upper_resid = passed_along(tail_residual, "strip", 1)
    lower_resid = passed_along(residual_all[:, :, :radius], "strip", -1)
    residual_wide = extend(upper_resid, residual_all, lower_resid, length, 2)

    across = jnp.einsum(
        "swjc,wkdc->kswjd", residual_wide, column_band, preferred_element_type=jnp.float32
    ).astype(jnp.bfloat16)
    adjoint = (
        jnp.einsum("wkij,kswjc->swic", row_back, across, preferred_element_type=jnp.float32)
        * rows_live[:, None]
    )

    def model_of(params_now):
        return stokes_model(params_now, wave_grid)

    def gradient_rows(first_row, row_count):
        params_rows = lax.dynamic_slice_in_dim(own_params, first_row, row_count, 1)
        adjoint_rows = lax.dynamic_slice_in_dim(adjoint, first_row, row_count, 2)
        unused_model, pullback = jax.vjp(model_of, params_rows)
        return pullback(adjoint_rows)[0]

    top_bit = wave_total // 2
    half_rows = capacity // 2
    high_side = ((wave_pos & top_bit) != 0).astype(jnp.int32)
    given = gradient_rows((1 - high_side) * half_rows, half_rows)
    kept = gradient_rows(high_side * half_rows, half_rows)
    merged = kept + exchange(given, "wave", top_bit)
    pieces = merged.reshape(
        merged.shape[0], top_bit, capacity // wave_total, columns
    ).transpose(1, 0, 2, 3)
    return scatter_by_halving(pieces, "wave", top_bit // 2).reshape(unit_params.shape)


def solution(mesh):
    return jax.shard_map(
        per_device,
        mesh=mesh,
        in_specs=(
            P(None, "strip", "wave"),
            P(None, "wave", "strip", None),
            P("wave", None, None),
            P("wave", None, None),
            P("strip", None),
            P("strip"),
        ),
        out_specs=P(None, "strip", "wave"),
        check_vma=False,
    )
```

```python
import jax
import jax.numpy as jnp
from jax import lax
from jax.sharding import PartitionSpec as P

parameter_low = (0.2, 0.4, 2.0, -0.8, 0.4, 0.3, 0.0, 0.0, 0.0)
parameter_span = (0.4, 0.6, 18.0, 1.6, 0.8, 1.2, 1.5, 3.141592653589793, 3.141592653589793)
stokes_weight = (1.0, 3.0, 3.0, 2.0)
loss_scale = 0.03125


def passed_along(shard, axis, by):
    count = lax.axis_size(axis)
    pairs = [(i, i + by) for i in range(count) if 0 <= i + by < count]
    return lax.ppermute(shard, axis, pairs)


def exchange(shard, axis, bit):
    count = lax.axis_size(axis)
    pairs = [(i, i ^ bit) for i in range(count)]
    return lax.ppermute(shard, axis, pairs)


def gather_by_doubling(shard, axis):
    count = lax.axis_size(axis)
    position = lax.axis_index(axis)
    bit = 1
    while bit < count:
        other = exchange(shard, axis, bit)
        low_side = (position & bit) == 0
        shard = jnp.where(
            low_side,
            jnp.concatenate([shard, other], axis=0),
            jnp.concatenate([other, shard], axis=0),
        )
        bit *= 2
    return shard


def scatter_by_halving(pieces, axis, bit):
    position = lax.axis_index(axis)
    while bit >= 1:
        half = pieces.shape[0] // 2
        high_side = ((position & bit) != 0).astype(jnp.int32)
        keep = lax.dynamic_slice_in_dim(pieces, high_side * half, half, 0)
        give = lax.dynamic_slice_in_dim(pieces, (1 - high_side) * half, half, 0)
        pieces = keep + exchange(give, axis, bit)
        bit //= 2
    return pieces[0]


def profile(distance, damping):
    scaled = distance / damping
    return 1.0 / (1.0 + scaled * scaled)


def stokes_model(unit_params, wave_grid):
    physical = [
        parameter_low[number] + parameter_span[number] * unit_params[number] for number in range(9)
    ]
    (
        source_zero,
        source_slope,
        strength,
        doppler,
        line_width,
        damping,
        zeeman_split,
        incline,
        azimuth,
    ) = physical
    offset = (wave_grid[:, None, None] - doppler) / line_width
    split_ratio = zeeman_split / line_width
    centre = profile(offset, damping)
    upper_line = profile(offset - split_ratio, damping)
    lower_line = profile(offset + split_ratio, damping)
    cosine = jnp.cos(incline)
    sine_value = jnp.sin(incline)
    sine_square = sine_value * sine_value
    absorb_total = 1.0 + strength * (
        centre * sine_square * 0.5 + (upper_line + lower_line) * (1.0 + cosine * cosine) * 0.25
    )
    linear = strength * (centre - 0.5 * (upper_line + lower_line)) * sine_square * 0.5
    linear_cosine = linear * jnp.cos(2.0 * azimuth)
    linear_sine = linear * jnp.sin(2.0 * azimuth)
    circular = strength * (lower_line - upper_line) * cosine * 0.5
    denominator = (
        absorb_total * absorb_total
        - linear_cosine * linear_cosine
        - linear_sine * linear_sine
        - circular * circular
    )
    source_ratio = source_slope / denominator
    return jnp.stack(
        [
            source_zero + source_ratio * absorb_total,
            -source_ratio * linear_cosine,
            -source_ratio * linear_sine,
            -source_ratio * circular,
        ]
    )


def band_tables(tap_table, out_rows, tap_count):
    in_rows = out_rows + tap_count - 1
    target_row = lax.broadcasted_iota(jnp.int32, (out_rows, in_rows, tap_count), 0)
    source_row = lax.broadcasted_iota(jnp.int32, (out_rows, in_rows, tap_count), 1)
    tap_index = lax.broadcasted_iota(jnp.int32, (out_rows, in_rows, tap_count), 2)
    selector = (source_row - target_row == tap_index).astype(jnp.bfloat16)
    return jnp.einsum(
        "wkt,ijt->wkij", tap_table, selector, preferred_element_type=jnp.float32
    ).astype(jnp.bfloat16)


def column_tables(tap_table, columns, tap_count):
    radius = tap_count // 2
    source_column = lax.broadcasted_iota(jnp.int32, (columns, columns, tap_count), 0)
    target_column = lax.broadcasted_iota(jnp.int32, (columns, columns, tap_count), 1)
    tap_index = lax.broadcasted_iota(jnp.int32, (columns, columns, tap_count), 2)
    selector = (source_column - target_column + radius == tap_index).astype(jnp.bfloat16)
    return jnp.einsum(
        "wkt,xyt->wkxy", tap_table, selector, preferred_element_type=jnp.float32
    ).astype(jnp.bfloat16)


def extend(upper_rim, middle, lower_rim, length, axis_index):
    radius = upper_rim.shape[axis_index]
    extent = middle.shape[axis_index]
    wide = extent + 2 * radius

    def padded(part, before, after):
        widths = [(0, 0)] * part.ndim
        widths[axis_index] = (before, after)
        return jnp.pad(part, widths)

    upper_part = padded(upper_rim, 0, wide - radius)
    middle_part = padded(middle, radius, radius)
    lower_pool = padded(lower_rim, wide, wide)
    lower_part = lax.dynamic_slice_in_dim(lower_pool, wide - radius - length, wide, axis_index)
    return upper_part + middle_part + lower_part


def per_device(unit_params, observed, psf_rows, psf_cols, pixel_mask, strip_lengths):
    stokes_count, wave_count, capacity, columns = observed.shape
    tap_count = psf_rows.shape[2]
    radius = tap_count // 2
    wave_total = lax.axis_size("wave")
    gathered = gather_by_doubling(unit_params.reshape(1, -1), "wave")
    own_params = (
        gathered.reshape(wave_total, unit_params.shape[0], capacity // wave_total, columns)
        .transpose(1, 0, 2, 3)
        .reshape(unit_params.shape[0], capacity, columns)
    )
    length = strip_lengths[0]
    wave_pos = lax.axis_index("wave")
    levels = (wave_pos * wave_count + jnp.arange(wave_count, dtype=jnp.int32)).astype(jnp.float32)
    wave_grid = -3.0 + 6.0 * levels / (wave_count * wave_total - 1)
    row_index = jnp.arange(capacity, dtype=jnp.int32)
    rows_live = (row_index < length).astype(jnp.float32)
    param_tail = lax.dynamic_slice_in_dim(own_params, length - radius, radius, 1)
    upper_params = passed_along(param_tail, "strip", 1)
    lower_params = passed_along(own_params[:, :radius], "strip", -1)
    strip_pos = lax.axis_index("strip")
    has_upper = strip_pos > 0
    has_lower = strip_pos < lax.axis_size("strip") - 1
    model_own = (stokes_model(own_params, wave_grid) * rows_live[:, None]).astype(jnp.bfloat16)
    upper_rim = jnp.where(has_upper, stokes_model(upper_params, wave_grid), 0.0).astype(jnp.bfloat16)
    lower_rim = jnp.where(has_lower, stokes_model(lower_params, wave_grid), 0.0).astype(jnp.bfloat16)
    model_wide = extend(upper_rim, model_own, lower_rim, length, 2)
    row_band = band_tables(psf_rows, capacity, tap_count)
    column_band = column_tables(psf_cols, columns, tap_count)
    live_mask = pixel_mask.astype(jnp.float32) * rows_live[:, None]
    weight_square = jnp.array(stokes_weight, jnp.float32)
    weight_square = weight_square * weight_square

    row_pass = jnp.einsum(
        "wkij,swjc->kswic", row_band, model_wide, preferred_element_type=jnp.float32
    ).astype(jnp.bfloat16)
    blurred = jnp.einsum(
        "kswic,wkcd->swid", row_pass, column_band, preferred_element_type=jnp.float32
    )
    residual_all = (
        loss_scale
        * weight_square[:, None, None, None]
        * live_mask
        * (blurred - observed.astype(jnp.float32))
    ).astype(jnp.bfloat16)

    row_back = band_tables(psf_rows[:, :, ::-1], capacity, tap_count)
    tail_residual = lax.dynamic_slice_in_dim(residual_all, length - radius, radius, 2)
    def passed_in_halves(rows, by):
        width = rows.shape[1] // 2
        first = passed_along(rows[:, :width], "strip", by)
        second = passed_along(rows[:, width:], "strip", by)
        return jnp.pad(first, ((0, 0), (0, width), (0, 0), (0, 0))) + jnp.pad(
            second, ((0, 0), (width, 0), (0, 0), (0, 0))
        )

    upper_resid = passed_in_halves(tail_residual, 1)
    lower_resid = passed_in_halves(residual_all[:, :, :radius], -1)
    residual_wide = extend(upper_resid, residual_all, lower_resid, length, 2)

    across = jnp.einsum(
        "swjc,wkdc->kswjd", residual_wide, column_band, preferred_element_type=jnp.float32
    ).astype(jnp.bfloat16)
    adjoint = (
        jnp.einsum("wkij,kswjc->swic", row_back, across, preferred_element_type=jnp.float32)
        * rows_live[:, None]
    )

    def model_of(params_now):
        return stokes_model(params_now, wave_grid)

    def gradient_rows(first_row, row_count):
        params_rows = lax.dynamic_slice_in_dim(own_params, first_row, row_count, 1)
        adjoint_rows = lax.dynamic_slice_in_dim(adjoint, first_row, row_count, 2)
        unused_model, pullback = jax.vjp(model_of, params_rows)
        return pullback(adjoint_rows)[0]

    top_bit = wave_total // 2
    half_rows = capacity // 2
    high_side = ((wave_pos & top_bit) != 0).astype(jnp.int32)
    given = gradient_rows((1 - high_side) * half_rows, half_rows)
    kept = gradient_rows(high_side * half_rows, half_rows)
    merged = kept + exchange(given, "wave", top_bit)
    pieces = merged.reshape(
        merged.shape[0], top_bit, capacity // wave_total, columns
    ).transpose(1, 0, 2, 3)
    return scatter_by_halving(pieces, "wave", top_bit // 2).reshape(unit_params.shape)


def solution(mesh):
    return jax.shard_map(
        per_device,
        mesh=mesh,
        in_specs=(
            P(None, "strip", "wave"),
            P(None, "wave", "strip", None),
            P("wave", None, None),
            P("wave", None, None),
            P("strip", None),
            P("strip"),
        ),
        out_specs=P(None, "strip", "wave"),
        check_vma=False,
    )
```

```python
import jax
import jax.numpy as jnp
from jax import lax
from jax.sharding import PartitionSpec as P

parameter_low = (0.2, 0.4, 2.0, -0.8, 0.4, 0.3, 0.0, 0.0, 0.0)
parameter_span = (0.4, 0.6, 18.0, 1.6, 0.8, 1.2, 1.5, 3.141592653589793, 3.141592653589793)
stokes_weight = (1.0, 3.0, 3.0, 2.0)
loss_scale = 0.03125


def passed_along(shard, axis, by):
    count = lax.axis_size(axis)
    pairs = [(i, i + by) for i in range(count) if 0 <= i + by < count]
    return lax.ppermute(shard, axis, pairs)


def exchange(shard, axis, bit):
    count = lax.axis_size(axis)
    pairs = [(i, i ^ bit) for i in range(count)]
    return lax.ppermute(shard, axis, pairs)


def gather_by_doubling(shard, axis):
    count = lax.axis_size(axis)
    position = lax.axis_index(axis)
    bit = 1
    while bit < count:
        other = exchange(shard, axis, bit)
        low_side = (position & bit) == 0
        shard = jnp.where(
            low_side,
            jnp.concatenate([shard, other], axis=0),
            jnp.concatenate([other, shard], axis=0),
        )
        bit *= 2
    return shard


def scatter_by_halving(pieces, axis, bit):
    position = lax.axis_index(axis)
    while bit >= 1:
        half = pieces.shape[0] // 2
        high_side = ((position & bit) != 0).astype(jnp.int32)
        keep = lax.dynamic_slice_in_dim(pieces, high_side * half, half, 0)
        give = lax.dynamic_slice_in_dim(pieces, (1 - high_side) * half, half, 0)
        pieces = keep + exchange(give, axis, bit)
        bit //= 2
    return pieces[0]


def profile(distance, damping):
    scaled = distance / damping
    return 1.0 / (1.0 + scaled * scaled)


def stokes_model(unit_params, wave_grid):
    physical = [
        parameter_low[number] + parameter_span[number] * unit_params[number] for number in range(9)
    ]
    (
        source_zero,
        source_slope,
        strength,
        doppler,
        line_width,
        damping,
        zeeman_split,
        incline,
        azimuth,
    ) = physical
    offset = (wave_grid[:, None, None] - doppler) / line_width
    split_ratio = zeeman_split / line_width
    centre = profile(offset, damping)
    upper_line = profile(offset - split_ratio, damping)
    lower_line = profile(offset + split_ratio, damping)
    cosine = jnp.cos(incline)
    sine_value = jnp.sin(incline)
    sine_square = sine_value * sine_value
    absorb_total = 1.0 + strength * (
        centre * sine_square * 0.5 + (upper_line + lower_line) * (1.0 + cosine * cosine) * 0.25
    )
    linear = strength * (centre - 0.5 * (upper_line + lower_line)) * sine_square * 0.5
    linear_cosine = linear * jnp.cos(2.0 * azimuth)
    linear_sine = linear * jnp.sin(2.0 * azimuth)
    circular = strength * (lower_line - upper_line) * cosine * 0.5
    denominator = (
        absorb_total * absorb_total
        - linear_cosine * linear_cosine
        - linear_sine * linear_sine
        - circular * circular
    )
    source_ratio = source_slope / denominator
    return jnp.stack(
        [
            source_zero + source_ratio * absorb_total,
            -source_ratio * linear_cosine,
            -source_ratio * linear_sine,
            -source_ratio * circular,
        ]
    )


def band_tables(tap_table, out_rows, tap_count):
    in_rows = out_rows + tap_count - 1
    target_row = lax.broadcasted_iota(jnp.int32, (out_rows, in_rows, tap_count), 0)
    source_row = lax.broadcasted_iota(jnp.int32, (out_rows, in_rows, tap_count), 1)
    tap_index = lax.broadcasted_iota(jnp.int32, (out_rows, in_rows, tap_count), 2)
    selector = (source_row - target_row == tap_index).astype(jnp.bfloat16)
    return jnp.einsum(
        "wkt,ijt->wkij", tap_table, selector, preferred_element_type=jnp.float32
    ).astype(jnp.bfloat16)


def column_tables(tap_table, columns, tap_count):
    radius = tap_count // 2
    source_column = lax.broadcasted_iota(jnp.int32, (columns, columns, tap_count), 0)
    target_column = lax.broadcasted_iota(jnp.int32, (columns, columns, tap_count), 1)
    tap_index = lax.broadcasted_iota(jnp.int32, (columns, columns, tap_count), 2)
    selector = (source_column - target_column + radius == tap_index).astype(jnp.bfloat16)
    return jnp.einsum(
        "wkt,xyt->wkxy", tap_table, selector, preferred_element_type=jnp.float32
    ).astype(jnp.bfloat16)


def extend(upper_rim, middle, lower_rim, length, axis_index):
    radius = upper_rim.shape[axis_index]
    extent = middle.shape[axis_index]
    wide = extent + 2 * radius

    def padded(part, before, after):
        widths = [(0, 0)] * part.ndim
        widths[axis_index] = (before, after)
        return jnp.pad(part, widths)

    upper_part = padded(upper_rim, 0, wide - radius)
    middle_part = padded(middle, radius, radius)
    lower_pool = padded(lower_rim, wide, wide)
    lower_part = lax.dynamic_slice_in_dim(lower_pool, wide - radius - length, wide, axis_index)
    return upper_part + middle_part + lower_part


def per_device(unit_params, observed, psf_rows, psf_cols, pixel_mask, strip_lengths):
    stokes_count, wave_count, capacity, columns = observed.shape
    tap_count = psf_rows.shape[2]
    radius = tap_count // 2
    wave_total = lax.axis_size("wave")
    gathered = gather_by_doubling(unit_params.reshape(1, -1), "wave")
    own_params = (
        gathered.reshape(wave_total, unit_params.shape[0], capacity // wave_total, columns)
        .transpose(1, 0, 2, 3)
        .reshape(unit_params.shape[0], capacity, columns)
    )
    length = strip_lengths[0]
    wave_pos = lax.axis_index("wave")
    levels = (wave_pos * wave_count + jnp.arange(wave_count, dtype=jnp.int32)).astype(jnp.float32)
    wave_grid = -3.0 + 6.0 * levels / (wave_count * wave_total - 1)
    row_index = jnp.arange(capacity, dtype=jnp.int32)
    rows_live = (row_index < length).astype(jnp.float32)
    param_tail = lax.dynamic_slice_in_dim(own_params, length - radius, radius, 1)
    upper_params = passed_along(param_tail, "strip", 1)
    lower_params = passed_along(own_params[:, :radius], "strip", -1)
    strip_pos = lax.axis_index("strip")
    has_upper = strip_pos > 0
    has_lower = strip_pos < lax.axis_size("strip") - 1
    model_own = (stokes_model(own_params, wave_grid) * rows_live[:, None]).astype(jnp.bfloat16)
    upper_rim = jnp.where(has_upper, stokes_model(upper_params, wave_grid), 0.0).astype(jnp.bfloat16)
    lower_rim = jnp.where(has_lower, stokes_model(lower_params, wave_grid), 0.0).astype(jnp.bfloat16)
    model_wide = extend(upper_rim, model_own, lower_rim, length, 2)
    row_band = band_tables(psf_rows, capacity, tap_count)
    column_band = column_tables(psf_cols, columns, tap_count)
    live_mask = pixel_mask.astype(jnp.float32) * rows_live[:, None]
    weight_square = jnp.array(stokes_weight, jnp.float32)
    weight_square = weight_square * weight_square

    row_pass = jnp.einsum(
        "wkij,swjc->kswic", row_band, model_wide, preferred_element_type=jnp.float32
    ).astype(jnp.bfloat16)
    blurred = jnp.einsum(
        "kswic,wkcd->swid", row_pass, column_band, preferred_element_type=jnp.float32
    )
    residual_all = (
        loss_scale
        * weight_square[:, None, None, None]
        * live_mask
        * (blurred - observed.astype(jnp.float32))
    ).astype(jnp.bfloat16)

    row_back = band_tables(psf_rows[:, :, ::-1], capacity, tap_count)
    tail_residual = lax.dynamic_slice_in_dim(residual_all, length - radius, radius, 2)
    upper_resid = passed_along(tail_residual, "strip", 1)
    lower_resid = passed_along(residual_all[:, :, :radius], "strip", -1)
    residual_wide = extend(upper_resid, residual_all, lower_resid, length, 2)

    across = jnp.einsum(
        "swjc,wkdc->kswjd", residual_wide, column_band, preferred_element_type=jnp.float32
    ).astype(jnp.bfloat16)
    adjoint = (
        jnp.einsum("wkij,kswjc->swic", row_back, across, preferred_element_type=jnp.float32)
        * rows_live[:, None]
    )

    def model_of(params_now):
        return stokes_model(params_now, wave_grid)

    def gradient_rows(first_row, row_count):
        params_rows = lax.dynamic_slice_in_dim(own_params, first_row, row_count, 1)
        adjoint_rows = lax.dynamic_slice_in_dim(adjoint, first_row, row_count, 2)
        unused_model, pullback = jax.vjp(model_of, params_rows)
        return pullback(adjoint_rows)[0]

    top_bit = wave_total // 2
    half_rows = capacity // 2
    quarter_rows = half_rows // 2
    high_side = ((wave_pos & top_bit) != 0).astype(jnp.int32)
    next_side = ((wave_pos & (top_bit // 2)) != 0).astype(jnp.int32)
    kept_first = high_side * half_rows
    given = gradient_rows((1 - high_side) * half_rows, half_rows)
    given_quarter = gradient_rows(kept_first + (1 - next_side) * quarter_rows, quarter_rows)
    kept_quarter = gradient_rows(kept_first + next_side * quarter_rows, quarter_rows)
    kept = jnp.where(
        next_side == 0,
        jnp.concatenate([kept_quarter, given_quarter], axis=1),
        jnp.concatenate([given_quarter, kept_quarter], axis=1),
    )
    merged = kept + exchange(given, "wave", top_bit)
    pieces = merged.reshape(
        merged.shape[0], top_bit, capacity // wave_total, columns
    ).transpose(1, 0, 2, 3)
    return scatter_by_halving(pieces, "wave", top_bit // 2).reshape(unit_params.shape)


def solution(mesh):
    return jax.shard_map(
        per_device,
        mesh=mesh,
        in_specs=(
            P(None, "strip", "wave"),
            P(None, "wave", "strip", None),
            P("wave", None, None),
            P("wave", None, None),
            P("strip", None),
            P("strip"),
        ),
        out_specs=P(None, "strip", "wave"),
        check_vma=False,
    )
```

```python
import jax
import jax.numpy as jnp
from jax import lax
from jax.sharding import PartitionSpec as P

parameter_low = (0.2, 0.4, 2.0, -0.8, 0.4, 0.3, 0.0, 0.0, 0.0)
parameter_span = (0.4, 0.6, 18.0, 1.6, 0.8, 1.2, 1.5, 3.141592653589793, 3.141592653589793)
stokes_weight = (1.0, 3.0, 3.0, 2.0)
loss_scale = 0.03125


def passed_along(shard, axis, by):
    count = lax.axis_size(axis)
    pairs = [(i, i + by) for i in range(count) if 0 <= i + by < count]
    return lax.ppermute(shard, axis, pairs)


def exchange(shard, axis, bit):
    count = lax.axis_size(axis)
    pairs = [(i, i ^ bit) for i in range(count)]
    return lax.ppermute(shard, axis, pairs)


def gather_by_doubling(shard, axis):
    count = lax.axis_size(axis)
    position = lax.axis_index(axis)
    bit = 1
    while bit < count:
        other = exchange(shard, axis, bit)
        low_side = (position & bit) == 0
        shard = jnp.where(
            low_side,
            jnp.concatenate([shard, other], axis=0),
            jnp.concatenate([other, shard], axis=0),
        )
        bit *= 2
    return shard


def scatter_by_halving(pieces, axis, bit):
    position = lax.axis_index(axis)
    while bit >= 1:
        half = pieces.shape[0] // 2
        high_side = ((position & bit) != 0).astype(jnp.int32)
        keep = lax.dynamic_slice_in_dim(pieces, high_side * half, half, 0)
        give = lax.dynamic_slice_in_dim(pieces, (1 - high_side) * half, half, 0)
        pieces = keep + exchange(give, axis, bit)
        bit //= 2
    return pieces[0]


def profile(distance, damping):
    scaled = distance / damping
    return 1.0 / (1.0 + scaled * scaled)


def stokes_model(unit_params, wave_grid):
    physical = [
        parameter_low[number] + parameter_span[number] * unit_params[number] for number in range(9)
    ]
    (
        source_zero,
        source_slope,
        strength,
        doppler,
        line_width,
        damping,
        zeeman_split,
        incline,
        azimuth,
    ) = physical
    offset = (wave_grid[:, None, None] - doppler) / line_width
    split_ratio = zeeman_split / line_width
    centre = profile(offset, damping)
    upper_line = profile(offset - split_ratio, damping)
    lower_line = profile(offset + split_ratio, damping)
    cosine = jnp.cos(incline)
    sine_value = jnp.sin(incline)
    sine_square = sine_value * sine_value
    absorb_total = 1.0 + strength * (
        centre * sine_square * 0.5 + (upper_line + lower_line) * (1.0 + cosine * cosine) * 0.25
    )
    linear = strength * (centre - 0.5 * (upper_line + lower_line)) * sine_square * 0.5
    linear_cosine = linear * jnp.cos(2.0 * azimuth)
    linear_sine = linear * jnp.sin(2.0 * azimuth)
    circular = strength * (lower_line - upper_line) * cosine * 0.5
    denominator = (
        absorb_total * absorb_total
        - linear_cosine * linear_cosine
        - linear_sine * linear_sine
        - circular * circular
    )
    source_ratio = source_slope / denominator
    return jnp.stack(
        [
            source_zero + source_ratio * absorb_total,
            -source_ratio * linear_cosine,
            -source_ratio * linear_sine,
            -source_ratio * circular,
        ]
    )


def band_tables(tap_table, out_rows, tap_count):
    in_rows = out_rows + tap_count - 1
    target_row = lax.broadcasted_iota(jnp.int32, (out_rows, in_rows, tap_count), 0)
    source_row = lax.broadcasted_iota(jnp.int32, (out_rows, in_rows, tap_count), 1)
    tap_index = lax.broadcasted_iota(jnp.int32, (out_rows, in_rows, tap_count), 2)
    selector = (source_row - target_row == tap_index).astype(jnp.bfloat16)
    return jnp.einsum(
        "wkt,ijt->wkij", tap_table, selector, preferred_element_type=jnp.float32
    ).astype(jnp.bfloat16)


def column_tables(tap_table, columns, tap_count):
    radius = tap_count // 2
    source_column = lax.broadcasted_iota(jnp.int32, (columns, columns, tap_count), 0)
    target_column = lax.broadcasted_iota(jnp.int32, (columns, columns, tap_count), 1)
    tap_index = lax.broadcasted_iota(jnp.int32, (columns, columns, tap_count), 2)
    selector = (source_column - target_column + radius == tap_index).astype(jnp.bfloat16)
    return jnp.einsum(
        "wkt,xyt->wkxy", tap_table, selector, preferred_element_type=jnp.float32
    ).astype(jnp.bfloat16)


def extend(upper_rim, middle, lower_rim, length, axis_index):
    radius = upper_rim.shape[axis_index]
    extent = middle.shape[axis_index]
    wide = extent + 2 * radius

    def padded(part, before, after):
        widths = [(0, 0)] * part.ndim
        widths[axis_index] = (before, after)
        return jnp.pad(part, widths)

    upper_part = padded(upper_rim, 0, wide - radius)
    middle_part = padded(middle, radius, radius)
    lower_pool = padded(lower_rim, wide, wide)
    lower_part = lax.dynamic_slice_in_dim(lower_pool, wide - radius - length, wide, axis_index)
    return upper_part + middle_part + lower_part


def per_device(unit_params, observed, psf_rows, psf_cols, pixel_mask, strip_lengths):
    stokes_count, wave_count, capacity, columns = observed.shape
    tap_count = psf_rows.shape[2]
    radius = tap_count // 2
    wave_total = lax.axis_size("wave")
    gathered = gather_by_doubling(unit_params.reshape(1, -1), "wave")
    own_params = (
        gathered.reshape(wave_total, unit_params.shape[0], capacity // wave_total, columns)
        .transpose(1, 0, 2, 3)
        .reshape(unit_params.shape[0], capacity, columns)
    )
    length = strip_lengths[0]
    wave_pos = lax.axis_index("wave")
    levels = (wave_pos * wave_count + jnp.arange(wave_count, dtype=jnp.int32)).astype(jnp.float32)
    wave_grid = -3.0 + 6.0 * levels / (wave_count * wave_total - 1)
    row_index = jnp.arange(capacity, dtype=jnp.int32)
    rows_live = (row_index < length).astype(jnp.float32)
    param_tail = lax.dynamic_slice_in_dim(own_params, length - radius, radius, 1)
    upper_params = passed_along(param_tail, "strip", 1)
    lower_params = passed_along(own_params[:, :radius], "strip", -1)
    strip_pos = lax.axis_index("strip")
    has_upper = strip_pos > 0
    has_lower = strip_pos < lax.axis_size("strip") - 1
    model_own = (stokes_model(own_params, wave_grid) * rows_live[:, None]).astype(jnp.bfloat16)
    upper_rim = jnp.where(has_upper, stokes_model(upper_params, wave_grid), 0.0).astype(jnp.bfloat16)
    lower_rim = jnp.where(has_lower, stokes_model(lower_params, wave_grid), 0.0).astype(jnp.bfloat16)
    model_wide = extend(upper_rim, model_own, lower_rim, length, 2)
    row_band = band_tables(psf_rows, capacity, tap_count)
    column_band = column_tables(psf_cols, columns, tap_count)
    live_mask = pixel_mask.astype(jnp.float32) * rows_live[:, None]
    weight_square = jnp.array(stokes_weight, jnp.float32)
    weight_square = weight_square * weight_square

    row_pass = jnp.einsum(
        "wkij,swjc->kswic", row_band, model_wide, preferred_element_type=jnp.float32
    ).astype(jnp.bfloat16)
    blurred = jnp.einsum(
        "kswic,wkcd->swid", row_pass, column_band, preferred_element_type=jnp.float32
    )
    residual_all = (
        loss_scale
        * weight_square[:, None, None, None]
        * live_mask
        * (blurred - observed.astype(jnp.float32))
    ).astype(jnp.bfloat16)

    row_back = band_tables(psf_rows[:, :, ::-1], capacity, tap_count)
    tail_residual = lax.dynamic_slice_in_dim(residual_all, length - radius, radius, 2)
    upper_resid = passed_along(tail_residual, "strip", 1)
    lower_resid = passed_along(residual_all[:, :, :radius], "strip", -1)
    residual_wide = extend(upper_resid, residual_all, lower_resid, length, 2)

    across = jnp.einsum(
        "swjc,wkdc->kswjd", residual_wide, column_band, preferred_element_type=jnp.float32
    ).astype(jnp.bfloat16)
    adjoint = (
        jnp.einsum("wkij,kswjc->swic", row_back, across, preferred_element_type=jnp.float32)
        * rows_live[:, None]
    )

    def model_of(params_now):
        return stokes_model(params_now, wave_grid)

    def gradient_rows(first_row, row_count):
        params_rows = lax.dynamic_slice_in_dim(own_params, first_row, row_count, 1)
        adjoint_rows = lax.dynamic_slice_in_dim(adjoint, first_row, row_count, 2)
        unused_model, pullback = jax.vjp(model_of, params_rows)
        return pullback(adjoint_rows)[0]

    bit = wave_total // 2
    span = capacity
    low_row = 0
    arrived = []
    sent = None
    while bit >= 1:
        span //= 2
        side = ((wave_pos & bit) != 0).astype(jnp.int32)
        give_row = low_row + (1 - side) * span
        if sent is not None:
            arrived.append(sent)
        part = gradient_rows(give_row, span)
        for first_row, received in arrived:
            part = part + lax.dynamic_slice_in_dim(received, give_row - first_row, span, 1)
        low_row = low_row + side * span
        sent = (low_row, exchange(part, "wave", bit))
        bit //= 2
    arrived.append(sent)
    own_part = gradient_rows(low_row, span)
    for first_row, received in arrived:
        own_part = own_part + lax.dynamic_slice_in_dim(received, low_row - first_row, span, 1)
    return own_part.reshape(unit_params.shape)


def solution(mesh):
    return jax.shard_map(
        per_device,
        mesh=mesh,
        in_specs=(
            P(None, "strip", "wave"),
            P(None, "wave", "strip", None),
            P("wave", None, None),
            P("wave", None, None),
            P("strip", None),
            P("strip"),
        ),
        out_specs=P(None, "strip", "wave"),
        check_vma=False,
    )
```
